32 devices in a mesh: dp: 8 (over y, x, core), seq: 4 (over z).
Axes of the slice: x: 2, y: 2, z: 4, core: 2. Of those that a mesh axis runs over, the one named last changes fastest.
Arguments:
- frames: bfloat16 [8, 12, 128, 1536], P('dp', 'seq'), may hold values from -17 to 17
- routes: int32 [8, 12], P('dp'), may hold values from 0 to 11, as said below
- lengths: int32 [8], P('dp'), may hold values from 384 to 1536
- attention_gain: float32 [1536], replicated, may hold values from 0.25 to 1.75
- query_weight: bfloat16 [1536, 768], P('dp'), may hold values from -1 to 1
- key_weight: bfloat16 [1536, 768], P('dp'), may hold values from -1.3 to 1.3
- value_weight: bfloat16 [1536, 768], P('dp'), may hold values from -0.15625 to 0.15625
- output_weight: bfloat16 [768, 1536], P('dp'), may hold values from -0.21875 to 0.21875
- convolution_gain: float32 [1536], replicated, may hold values from 0.25 to 1.75
- pointwise_in: bfloat16 [1536, 3072], P('dp'), may hold values from -0.15625 to 0.15625
- depthwise_taps: bfloat16 [31, 1536], replicated, may hold values from -1 to 1
- depthwise_gain: float32 [1536], replicated, may hold values from 0.25 to 1.75
- pointwise_out: bfloat16 [1536, 1536], P('dp'), may hold values from -0.15625 to 0.15625
Outputs:
- encoded: bfloat16 [8, 12, 128, 1536], P('dp', 'seq')
The draws below stay inside these ranges and needn't reach their ends.
Inputs may be any that keep to these rules, and one draw needn't show every extreme that they name: For each utterance, routes is a permutation of 0 to 11; the 3 sampler blocks b = r * 3 to r * 3 + 2 have routes[u, b] // 3 all different.
All inputs are finite; a program needn't handle non-finite values.
Results may differ from the reference program's by a relative error of at most 0.0074.
Values may be sent and summed in bfloat16 or wider, within the bound.
No kernel may reach another device: no remote copies, remote signals or barrier semaphores. Data moves between devices by JAX's collectives and lax.ppermute only.
A program may use at most 128 MiB of HBM per device.

```python
import math
import jax
import jax.numpy as jnp
from jax import lax

D = 1536
HEADS = 12
HEAD_DIM = 64
KERNEL = 31
BLOCK = 128
SHARD_BLOCKS = 3
ATT_WIDTH = 768
SEQS = 8
BLOCKS = 12
FRAMES = 1536


def draw_frames(key, part):
    shape = (SEQS, BLOCKS, BLOCK, D)
    return jnp.clip(jax.random.normal(key, shape, jnp.float32), -6.0, 6.0).astype(jnp.bfloat16)


def projection_pair(key):
    first = jnp.clip(jax.random.normal(jax.random.fold_in(key, 11), (D, HEADS * HEAD_DIM), jnp.float32), -6.0, 6.0)
    second = jnp.clip(jax.random.normal(jax.random.fold_in(key, 12), (D, HEADS * HEAD_DIM), jnp.float32), -6.0, 6.0)
    factor = 1.4 / D ** 0.5
    return (jnp.clip(factor * first, -1.0, 1.0), jnp.clip(factor * second, -1.3, 1.3))


def draw_query_weight(key, part):
    return projection_pair(key)[0].astype(jnp.bfloat16)


def draw_key_weight(key, part):
    return projection_pair(key)[1].astype(jnp.bfloat16)


def draw_routes(key, part):
    shards = BLOCKS // SHARD_BLOCKS
    listed = []
    for member in range(SEQS):
        member_key = jax.random.fold_in(key, member)
        offsets = jax.random.permutation(jax.random.fold_in(member_key, 1), shards)[:SHARD_BLOCKS]
        slot_map = jax.random.permutation(jax.random.fold_in(member_key, 2), SHARD_BLOCKS)
        picked = jnp.stack([jax.random.permutation(jax.random.fold_in(member_key, 10 + source), SHARD_BLOCKS) for source in range(shards)])
        source_ids = jnp.arange(shards)[:, None]
        target = (source_ids + offsets[picked]) % shards
        places = target * SHARD_BLOCKS + slot_map[picked]
        listed.append(places.reshape(-1))
    return jnp.stack(listed).astype(jnp.int32)


def plant(drawn, rng, least, largest):
    shape = drawn.shape
    spot = [jax.random.randint(jax.random.fold_in(rng, axis), (), 0, shape[axis]) for axis in range(len(shape))]
    drawn = drawn.at[tuple(spot)].set(least)
    longest = shape.index(max(shape))
    spot[longest] = (spot[longest] + 1) % shape[longest]
    return drawn.at[tuple(spot)].set(largest)


def level_of(rng, dims, split, smallest, high):
    loudness = 1.0
    for position, parts in split:
        draws = jax.random.uniform(jax.random.fold_in(jax.random.fold_in(rng, 6), position), (parts,), jnp.float32, smallest / len(split), high / len(split))
        loudness = loudness * jnp.repeat(jnp.exp(draws), dims[position] // parts).reshape((-1,) + (1,) * (len(dims) - 1 - position))
    return loudness


def noise(key, dims, deviation, bound, cuts=(), kind=jnp.bfloat16):
    values = deviation * jax.random.normal(key, dims, jnp.float32)
    if cuts:
        values = values * level_of(key, dims, cuts, -0.22, 0.18)
    return jnp.clip(values, -bound, bound).astype(kind)


def setup_inputs(seed: int = 0) -> dict:
    streams_of = jax.random.split(jax.random.key(seed), 14)
    frames = draw_frames(jax.random.fold_in(streams_of[13], 71), 0)
    routes = draw_routes(jax.random.fold_in(streams_of[13], 71), 0)
    lengths = plant(jax.random.randint(streams_of[2], (SEQS,), FRAMES // 4, FRAMES + 1), jax.random.fold_in(streams_of[2], 1), FRAMES // 4, FRAMES).astype(jnp.int32)
    attention_gain = jnp.clip(1.0 + 0.15 * jax.random.normal(streams_of[3], (D,), jnp.float32), 0.25, 1.75)
    query_weight = draw_query_weight(jax.random.fold_in(streams_of[13], 71), 0)
    key_weight = draw_key_weight(jax.random.fold_in(streams_of[13], 71), 0)
    value_weight = noise(streams_of[6], (D, ATT_WIDTH), D ** -0.5, 0.15625, ((0, 8),))
    output_weight = noise(streams_of[7], (ATT_WIDTH, D), ATT_WIDTH ** -0.5, 0.21875, ((0, 8),))
    convolution_gain = jnp.clip(1.0 + 0.15 * jax.random.normal(streams_of[8], (D,), jnp.float32), 0.25, 1.75)
    pointwise_in = noise(streams_of[9], (D, 2 * D), D ** -0.5, 0.15625, ((0, 8),))
    depthwise_taps = noise(streams_of[10], (KERNEL, D), KERNEL ** -0.5, 1.0)
    depthwise_gain = jnp.clip(1.0 + 0.15 * jax.random.normal(streams_of[11], (D,), jnp.float32), 0.25, 1.75)
    pointwise_out = noise(streams_of[12], (D, D), D ** -0.5, 0.15625, ((0, 8),))
    return dict(frames=frames, routes=routes, lengths=lengths, attention_gain=attention_gain, query_weight=query_weight, key_weight=key_weight, value_weight=value_weight, output_weight=output_weight, convolution_gain=convolution_gain, pointwise_in=pointwise_in, depthwise_taps=depthwise_taps, depthwise_gain=depthwise_gain, pointwise_out=pointwise_out)


def layer_norm(values, gain_row):
    values = values.astype(jnp.float32)
    center = values - lax.optimization_barrier(jnp.mean(values, axis=-1, keepdims=True))
    spread = lax.optimization_barrier(jnp.mean(center * center, axis=-1, keepdims=True))
    return center * lax.rsqrt(spread + 1e-05) * gain_row.astype(jnp.float32)

def encode_utterance(ordered, length, attention_gain, query_weight, key_weight, value_weight, output_weight, convolution_gain, pointwise_in, depthwise_taps, depthwise_gain, pointwise_out):
    frame_count = ordered.shape[0]
    is_valid = jnp.arange(frame_count) < length
    normed = layer_norm(ordered, attention_gain).astype(jnp.bfloat16)
    queries = jnp.dot(normed, query_weight, preferred_element_type=jnp.float32).astype(jnp.bfloat16)
    key_rows = jnp.dot(normed, key_weight, preferred_element_type=jnp.float32).astype(jnp.bfloat16)
    value_rows = jnp.dot(normed, value_weight, preferred_element_type=jnp.float32).astype(jnp.bfloat16)
    scaling = 1.0 / math.sqrt(HEAD_DIM)

    def head_attention(items):
        query_head, key_head, value_head = items
        scores = jnp.dot(query_head, key_head.T, preferred_element_type=jnp.float32) * scaling
        scores = jnp.where(is_valid[None, :], scores, -1e+30)
        top = lax.optimization_barrier(jnp.max(scores, axis=1, keepdims=True))
        weights_exp = jnp.where(is_valid[None, :], jnp.exp(scores - top), 0.0)
        numer = jnp.dot(weights_exp.astype(jnp.bfloat16), value_head, preferred_element_type=jnp.float32)
        return numer / lax.optimization_barrier(jnp.sum(weights_exp, axis=1, keepdims=True))

    def split_heads(matrix):
        return matrix.reshape(frame_count, HEADS, HEAD_DIM).transpose(1, 0, 2)
    mixed = lax.map(head_attention, (split_heads(queries), split_heads(key_rows), split_heads(value_rows)))
    attended = mixed.transpose(1, 0, 2).reshape(frame_count, HEADS * HEAD_DIM).astype(jnp.bfloat16)
    after_attn = (ordered.astype(jnp.float32) + jnp.dot(attended, output_weight, preferred_element_type=jnp.float32)).astype(jnp.bfloat16)
    conv_normed = layer_norm(after_attn, convolution_gain).astype(jnp.bfloat16)
    expanded = jnp.dot(conv_normed, pointwise_in, preferred_element_type=jnp.float32)
    width = ordered.shape[1]
    gated = expanded[:, :width] * jax.nn.sigmoid(expanded[:, width:])
    gated = jnp.where(is_valid[:, None], gated, 0.0).astype(jnp.bfloat16)
    half = KERNEL // 2
    padded = jnp.pad(gated.astype(jnp.float32), ((half, half), (0, 0)))
    depthwise = jnp.zeros((frame_count, width), jnp.float32)
    for tap in range(KERNEL):
        depthwise = depthwise + depthwise_taps[tap].astype(jnp.float32)[None, :] * padded[tap:tap + frame_count]
    shaped = layer_norm(depthwise, depthwise_gain)
    activated = (shaped * jax.nn.sigmoid(shaped)).astype(jnp.bfloat16)
    return (after_attn.astype(jnp.float32) + jnp.dot(activated, pointwise_out, preferred_element_type=jnp.float32)).astype(jnp.bfloat16)

def reference(frames, routes, lengths, attention_gain, query_weight, key_weight, value_weight, output_weight, convolution_gain, pointwise_in, depthwise_taps, depthwise_gain, pointwise_out):

    def one_utterance(items):
        blocks, route_row, length = items
        placed = jnp.zeros_like(blocks).at[route_row.astype(jnp.int32)].set(blocks)
        ordered = placed.reshape(BLOCKS * BLOCK, D)
        result = encode_utterance(ordered, length, attention_gain, query_weight, key_weight, value_weight, output_weight, convolution_gain, pointwise_in, depthwise_taps, depthwise_gain, pointwise_out)
        return result.reshape(BLOCKS, BLOCK, D)[route_row.astype(jnp.int32)]
    return lax.map(one_utterance, (frames, routes, lengths))
```

```python
import math

import jax
import jax.numpy as jnp
from jax import lax
from jax.sharding import PartitionSpec as P

HEAD_DIM = 64
KERNEL = 31
EDGE = 16


def layer_norm(values, gain_row):
    values = values.astype(jnp.float32)
    center = values - jnp.mean(values, axis=-1, keepdims=True)
    spread = jnp.mean(center * center, axis=-1, keepdims=True)
    return center * lax.rsqrt(spread + 1e-05) * gain_row


def select_blocks(selector, blocks):
    return jnp.einsum(
        "ab,bfc->afc", selector.astype(jnp.bfloat16), blocks, preferred_element_type=jnp.float32
    ).astype(jnp.bfloat16)


def add_rows(left, piece):
    return jnp.dot(left, piece, preferred_element_type=jnp.float32)


def body(
    frames,
    routes,
    lengths,
    attention_gain,
    query_weight,
    key_weight,
    value_weight,
    output_weight,
    convolution_gain,
    pointwise_in,
    depthwise_taps,
    depthwise_gain,
    pointwise_out,
):
    shard_index = lax.axis_index("seq")
    blocks_here = frames.shape[1]
    block_rows = frames.shape[2]
    width = frames.shape[3]
    frame_rows = blocks_here * block_rows
    route_row = routes[0]
    own_places = lax.dynamic_slice_in_dim(route_row, shard_index * blocks_here, blocks_here)
    length = lengths[0]
    ordered = frames[0].reshape(frame_rows, width)
    positions = (own_places[:, None] * block_rows + jnp.arange(block_rows)[None, :]).reshape(
        frame_rows
    )
    is_valid = positions < length
    normed = layer_norm(ordered, attention_gain).astype(jnp.bfloat16)
    att_width = query_weight.shape[1]
    qkv_local = jnp.concatenate([query_weight, key_weight, value_weight], axis=1)
    qkv_weight = lax.all_gather(qkv_local, "dp", axis=0, tiled=True)
    projected_qkv = add_rows(normed, qkv_weight).astype(jnp.bfloat16)
    queries = projected_qkv[:, :att_width]
    kv_rows = projected_qkv[:, att_width:]
    head_count = att_width // HEAD_DIM
    scaling = 1.0 / math.sqrt(HEAD_DIM)
    query_heads = queries.reshape(frame_rows, head_count, HEAD_DIM)
    start_top = jnp.full((head_count, frame_rows), -1e30, jnp.float32)
    start_total = jnp.zeros((head_count, frame_rows), jnp.float32)
    start_accum = jnp.zeros((frame_rows, head_count, HEAD_DIM), jnp.float32)
    carry = (start_top, start_total, start_accum)
    kv_piece = lax.all_gather(kv_rows, "seq", axis=0, tiled=True)
    key_piece = kv_piece[:, :att_width]
    value_piece = kv_piece[:, att_width:]
    key_count = key_piece.shape[0]
    key_positions = (
        route_row[:, None] * block_rows + jnp.arange(block_rows)[None, :]
    ).reshape(key_count)
    key_valid_all = key_positions < length
    chunk = 4 * block_rows
    for offset in range(0, key_count, chunk):
        stop = min(offset + chunk, key_count)
        key_block = key_piece[offset:stop].reshape(stop - offset, head_count, HEAD_DIM)
        value_block = value_piece[offset:stop].reshape(stop - offset, head_count, HEAD_DIM)
        key_valid = key_valid_all[offset:stop]

        def update(state, key_block=key_block, value_block=value_block, key_valid=key_valid):
            top_old, total_old, accum_old = state
            scores = (
                jnp.einsum(
                    "qhd,khd->hqk", query_heads, key_block, preferred_element_type=jnp.float32
                )
                * scaling
            )
            scores = jnp.where(key_valid[None, None, :], scores, -1e30)
            top_new = jnp.maximum(top_old, jnp.max(scores, axis=2))
            rescale = jnp.exp(top_old - top_new)
            weights_exp = jnp.where(
                key_valid[None, None, :], jnp.exp(scores - top_new[:, :, None]), 0.0
            )
            total_new = total_old * rescale + jnp.sum(weights_exp, axis=2)
            added = jnp.einsum(
                "hqk,khd->qhd",
                weights_exp.astype(jnp.bfloat16),
                value_block,
                preferred_element_type=jnp.float32,
            )
            accum_new = accum_old * rescale.T[:, :, None] + added
            return (top_new, total_new, accum_new)

        carry = update(carry)
    top_all, total_all, accum_all = carry
    attended = (
        (accum_all / total_all.T[:, :, None]).reshape(frame_rows, att_width).astype(jnp.bfloat16)
    )
    out_rows = output_weight.shape[0]
    in_width = pointwise_in.shape[1]
    late_local = jnp.concatenate(
        [
            output_weight.reshape(pointwise_in.shape[0], -1),
            pointwise_in,
            pointwise_out,
        ],
        axis=1,
    )
    late_weight = lax.all_gather(late_local, "dp", axis=0, tiled=True)
    out_cols = late_local.shape[1] - in_width - pointwise_out.shape[1]
    output_full = late_weight[:, :out_cols].reshape(-1, width)
    in_full = late_weight[:, out_cols : out_cols + in_width]
    out_full = late_weight[:, out_cols + in_width :]
    del out_rows
    projected = add_rows(attended, output_full)
    after_attn = (ordered.astype(jnp.float32) + projected).astype(jnp.bfloat16)
    conv_normed = layer_norm(after_attn, convolution_gain).astype(jnp.bfloat16)
    expanded = add_rows(conv_normed, in_full)
    gated = expanded[:, :width] * jax.nn.sigmoid(expanded[:, width:])
    gated = jnp.where(is_valid[:, None], gated, 0.0).astype(jnp.bfloat16)
    half = KERNEL // 2
    gated_blocks = gated.reshape(blocks_here, block_rows, width)
    edges = jnp.concatenate(
        [gated_blocks[:, :EDGE], gated_blocks[:, block_rows - EDGE :]], axis=1
    )
    all_edges = lax.all_gather(edges, "seq", axis=0, tiled=True)
    before = route_row[None, :] == (own_places[:, None] - 1)
    after = route_row[None, :] == (own_places[:, None] + 1)
    low = select_blocks(before, all_edges[:, EDGE:])[:, EDGE - half :]
    high = select_blocks(after, all_edges[:, :EDGE])[:, :half]
    padded = jnp.concatenate([low, gated_blocks, high], axis=1)
    depthwise = jnp.zeros((blocks_here, block_rows, width), jnp.float32)
    for tap in range(KERNEL):
        depthwise = depthwise + depthwise_taps[tap].astype(jnp.float32)[None, None, :] * padded[
            :, tap : tap + block_rows
        ].astype(jnp.float32)
    shaped = layer_norm(depthwise.reshape(frame_rows, width), depthwise_gain)
    activated = (shaped * jax.nn.sigmoid(shaped)).astype(jnp.bfloat16)
    contracted = add_rows(activated, out_full)
    result = (after_attn.astype(jnp.float32) + contracted).astype(jnp.bfloat16)
    return result.reshape(blocks_here, block_rows, width)[None]


def solution(mesh):
    placed = (
        P("dp", "seq", None, None),
        P("dp", None),
        P("dp"),
        P(),
        P("dp", None),
        P("dp", None),
        P("dp", None),
        P("dp", None),
        P(),
        P("dp", None),
        P(),
        P(),
        P("dp", None),
    )
    return jax.shard_map(
        body, mesh=mesh, in_specs=placed, out_specs=P("dp", "seq", None, None), check_vma=False
    )
```

```python
import math

import jax
import jax.numpy as jnp
from jax import lax
from jax.sharding import PartitionSpec as P

HEAD_DIM = 64
KERNEL = 31
EDGE = 16


def layer_norm(values, gain_row):
    values = values.astype(jnp.float32)
    center = values - jnp.mean(values, axis=-1, keepdims=True)
    spread = jnp.mean(center * center, axis=-1, keepdims=True)
    return center * lax.rsqrt(spread + 1e-05) * gain_row


def select_blocks(selector, blocks):
    return jnp.einsum(
        "ab,bfc->afc", selector.astype(jnp.bfloat16), blocks, preferred_element_type=jnp.float32
    ).astype(jnp.bfloat16)


def add_rows(left, piece):
    return jnp.dot(left, piece, preferred_element_type=jnp.float32)


def body(
    frames,
    routes,
    lengths,
    attention_gain,
    query_weight,
    key_weight,
    value_weight,
    output_weight,
    convolution_gain,
    pointwise_in,
    depthwise_taps,
    depthwise_gain,
    pointwise_out,
):
    shard_index = lax.axis_index("seq")
    blocks_here = frames.shape[1]
    block_rows = frames.shape[2]
    width = frames.shape[3]
    frame_rows = blocks_here * block_rows
    route_row = routes[0]
    own_places = lax.dynamic_slice_in_dim(route_row, shard_index * blocks_here, blocks_here)
    length = lengths[0]
    ordered = frames[0].reshape(frame_rows, width)
    positions = (own_places[:, None] * block_rows + jnp.arange(block_rows)[None, :]).reshape(
        frame_rows
    )
    is_valid = positions < length
    normed = layer_norm(ordered, attention_gain).astype(jnp.bfloat16)
    att_width = query_weight.shape[1]
    qkv_local = jnp.concatenate([query_weight, key_weight, value_weight], axis=1)
    qkv_weight = lax.all_gather(qkv_local, "dp", axis=0, tiled=True)
    projected_qkv = add_rows(normed, qkv_weight).astype(jnp.bfloat16)
    head_count = att_width // HEAD_DIM
    shards = lax.axis_size("seq")
    slots = -(-head_count // shards)
    scaling = 1.0 / math.sqrt(HEAD_DIM)
    qkv_heads = projected_qkv.reshape(frame_rows, 3, head_count, HEAD_DIM)
    qkv_heads = jnp.pad(
        qkv_heads, ((0, 0), (0, 0), (0, slots * shards - head_count), (0, 0))
    ).reshape(frame_rows, 3, slots, shards, HEAD_DIM)
    outbound = qkv_heads.transpose(3, 0, 1, 2, 4)
    arrived = lax.all_to_all(outbound, "seq", split_axis=0, concat_axis=0, tiled=True)
    all_rows = shards * frame_rows
    arrived = arrived.reshape(all_rows, 3, slots, HEAD_DIM)
    query_all = arrived[:, 0]
    key_all = arrived[:, 1]
    value_all = arrived[:, 2]
    key_positions = (
        route_row[:, None] * block_rows + jnp.arange(block_rows)[None, :]
    ).reshape(all_rows)
    key_valid = key_positions < length
    pieces = []
    chunk = 4 * block_rows
    for offset in range(0, all_rows, chunk):
        stop = min(offset + chunk, all_rows)
        scores = (
            jnp.einsum(
                "qhd,khd->hqk",
                query_all[offset:stop],
                key_all,
                preferred_element_type=jnp.float32,
            )
            * scaling
        )
        scores = jnp.where(key_valid[None, None, :], scores, -1e30)
        top = jnp.max(scores, axis=2, keepdims=True)
        weights_exp = jnp.where(key_valid[None, None, :], jnp.exp(scores - top), 0.0)
        numer = jnp.einsum(
            "hqk,khd->qhd",
            weights_exp.astype(jnp.bfloat16),
            value_all,
            preferred_element_type=jnp.float32,
        )
        total = jnp.sum(weights_exp, axis=2)
        pieces.append((numer / total.T[:, :, None]).astype(jnp.bfloat16))
    mixed = jnp.concatenate(pieces, axis=0).reshape(shards, frame_rows, slots, HEAD_DIM)
    returned = lax.all_to_all(mixed, "seq", split_axis=0, concat_axis=0, tiled=True)
    attended = returned.transpose(1, 2, 0, 3).reshape(frame_rows, slots * shards * HEAD_DIM)
    attended = attended[:, :att_width]
    out_rows = output_weight.shape[0]
    in_width = pointwise_in.shape[1]
    late_local = jnp.concatenate(
        [
            output_weight.reshape(pointwise_in.shape[0], -1),
            pointwise_in,
            pointwise_out,
        ],
        axis=1,
    )
    late_weight = lax.all_gather(late_local, "dp", axis=0, tiled=True)
    out_cols = late_local.shape[1] - in_width - pointwise_out.shape[1]
    output_full = late_weight[:, :out_cols].reshape(-1, width)
    in_full = late_weight[:, out_cols : out_cols + in_width]
    out_full = late_weight[:, out_cols + in_width :]
    del out_rows
    projected = add_rows(attended, output_full)
    after_attn = (ordered.astype(jnp.float32) + projected).astype(jnp.bfloat16)
    conv_normed = layer_norm(after_attn, convolution_gain).astype(jnp.bfloat16)
    expanded = add_rows(conv_normed, in_full)
    gated = expanded[:, :width] * jax.nn.sigmoid(expanded[:, width:])
    gated = jnp.where(is_valid[:, None], gated, 0.0).astype(jnp.bfloat16)
    half = KERNEL // 2
    gated_blocks = gated.reshape(blocks_here, block_rows, width)
    edges = jnp.concatenate(
        [gated_blocks[:, :EDGE], gated_blocks[:, block_rows - EDGE :]], axis=1
    )
    all_edges = lax.all_gather(edges, "seq", axis=0, tiled=True)
    before = route_row[None, :] == (own_places[:, None] - 1)
    after = route_row[None, :] == (own_places[:, None] + 1)
    low = select_blocks(before, all_edges[:, EDGE:])[:, EDGE - half :]
    high = select_blocks(after, all_edges[:, :EDGE])[:, :half]
    padded = jnp.concatenate([low, gated_blocks, high], axis=1)
    depthwise = jnp.zeros((blocks_here, block_rows, width), jnp.float32)
    for tap in range(KERNEL):
        depthwise = depthwise + depthwise_taps[tap].astype(jnp.float32)[None, None, :] * padded[
            :, tap : tap + block_rows
        ].astype(jnp.float32)
    shaped = layer_norm(depthwise.reshape(frame_rows, width), depthwise_gain)
    activated = (shaped * jax.nn.sigmoid(shaped)).astype(jnp.bfloat16)
    contracted = add_rows(activated, out_full)
    result = (after_attn.astype(jnp.float32) + contracted).astype(jnp.bfloat16)
    return result.reshape(blocks_here, block_rows, width)[None]


def solution(mesh):
    placed = (
        P("dp", "seq", None, None),
        P("dp", None),
        P("dp"),
        P(),
        P("dp", None),
        P("dp", None),
        P("dp", None),
        P("dp", None),
        P(),
        P("dp", None),
        P(),
        P(),
        P("dp", None),
    )
    return jax.shard_map(
        body, mesh=mesh, in_specs=placed, out_specs=P("dp", "seq", None, None), check_vma=False
    )
```

```python
import math

import jax
import jax.numpy as jnp
from jax import lax
from jax.sharding import PartitionSpec as P

HEAD_DIM = 64
KERNEL = 31
EDGE = 16


def layer_norm(values, gain_row):
    values = values.astype(jnp.float32)
    center = values - jnp.mean(values, axis=-1, keepdims=True)
    spread = jnp.mean(center * center, axis=-1, keepdims=True)
    return center * lax.rsqrt(spread + 1e-05) * gain_row


def select_blocks(selector, blocks):
    return jnp.einsum(
        "ab,bfc->afc", selector.astype(jnp.bfloat16), blocks, preferred_element_type=jnp.float32
    ).astype(jnp.bfloat16)


def add_rows(left, piece):
    return jnp.dot(left, piece, preferred_element_type=jnp.float32)


def body(
    frames,
    routes,
    lengths,
    attention_gain,
    query_weight,
    key_weight,
    value_weight,
    output_weight,
    convolution_gain,
    pointwise_in,
    depthwise_taps,
    depthwise_gain,
    pointwise_out,
):
    shard_index = lax.axis_index("seq")
    blocks_here = frames.shape[1]
    block_rows = frames.shape[2]
    width = frames.shape[3]
    frame_rows = blocks_here * block_rows
    route_row = routes[0]
    own_places = lax.dynamic_slice_in_dim(route_row, shard_index * blocks_here, blocks_here)
    length = lengths[0]
    ordered = frames[0].reshape(frame_rows, width)
    positions = (own_places[:, None] * block_rows + jnp.arange(block_rows)[None, :]).reshape(
        frame_rows
    )
    is_valid = positions < length
    normed = layer_norm(ordered, attention_gain).astype(jnp.bfloat16)
    att_width = query_weight.shape[1]
    qkv_local = jnp.concatenate([query_weight, key_weight, value_weight], axis=1)
    qkv_weight = lax.all_gather(qkv_local, "dp", axis=0, tiled=True)
    projected_qkv = add_rows(normed, qkv_weight).astype(jnp.bfloat16)
    head_count = att_width // HEAD_DIM
    shards = lax.axis_size("seq")
    slots = -(-head_count // shards)
    scaling = 1.0 / math.sqrt(HEAD_DIM)
    qkv_heads = projected_qkv.reshape(frame_rows, 3, head_count, HEAD_DIM)
    qkv_heads = jnp.pad(
        qkv_heads, ((0, 0), (0, 0), (0, slots * shards - head_count), (0, 0))
    ).reshape(frame_rows, 3, slots, shards, HEAD_DIM)
    all_rows = shards * frame_rows
    key_positions = (
        route_row[:, None] * block_rows + jnp.arange(block_rows)[None, :]
    ).reshape(all_rows)
    key_valid = key_positions < length
    chunk = 4 * block_rows
    slot_outputs = []
    inbound = [
        lax.all_to_all(
            qkv_heads[:, :, slot].transpose(2, 0, 1, 3),
            "seq",
            split_axis=0,
            concat_axis=0,
            tiled=True,
        )
        for slot in range(slots)
    ]
    previous = None
    for slot in range(slots):
        arrived = inbound[slot]
        if previous is not None:
            previous, arrived = lax.optimization_barrier((previous, arrived))
            slot_outputs[-1] = previous
        arrived = arrived.reshape(all_rows, 3, HEAD_DIM)
        query_all = arrived[:, 0]
        key_all = arrived[:, 1]
        value_all = arrived[:, 2]
        pieces = []
        for offset in range(0, all_rows, chunk):
            stop = min(offset + chunk, all_rows)
            scores = (
                jnp.dot(query_all[offset:stop], key_all.T, preferred_element_type=jnp.float32)
                * scaling
            )
            scores = jnp.where(key_valid[None, :], scores, -1e30)
            top = jnp.max(scores, axis=1, keepdims=True)
            weights_exp = jnp.where(key_valid[None, :], jnp.exp(scores - top), 0.0)
            numer = jnp.dot(
                weights_exp.astype(jnp.bfloat16), value_all, preferred_element_type=jnp.float32
            )
            total = jnp.sum(weights_exp, axis=1, keepdims=True)
            pieces.append((numer / total).astype(jnp.bfloat16))
        mixed = jnp.concatenate(pieces, axis=0).reshape(shards, frame_rows, HEAD_DIM)
        slot_outputs.append(mixed)
        previous = mixed
    slot_outputs = [
        lax.all_to_all(mixed, "seq", split_axis=0, concat_axis=0, tiled=True)
        for mixed in slot_outputs
    ]
    returned = jnp.stack(slot_outputs, axis=0)
    attended = returned.transpose(2, 0, 1, 3).reshape(frame_rows, slots * shards * HEAD_DIM)
    attended = attended[:, :att_width]
    out_rows = output_weight.shape[0]
    in_width = pointwise_in.shape[1]
    late_local = jnp.concatenate(
        [
            output_weight.reshape(pointwise_in.shape[0], -1),
            pointwise_in,
            pointwise_out,
        ],
        axis=1,
    )
    late_weight = lax.all_gather(late_local, "dp", axis=0, tiled=True)
    out_cols = late_local.shape[1] - in_width - pointwise_out.shape[1]
    output_full = late_weight[:, :out_cols].reshape(-1, width)
    in_full = late_weight[:, out_cols : out_cols + in_width]
    out_full = late_weight[:, out_cols + in_width :]
    del out_rows
    projected = add_rows(attended, output_full)
    after_attn = (ordered.astype(jnp.float32) + projected).astype(jnp.bfloat16)
    conv_normed = layer_norm(after_attn, convolution_gain).astype(jnp.bfloat16)
    expanded = add_rows(conv_normed, in_full)
    gated = expanded[:, :width] * jax.nn.sigmoid(expanded[:, width:])
    gated = jnp.where(is_valid[:, None], gated, 0.0).astype(jnp.bfloat16)
    half = KERNEL // 2
    gated_blocks = gated.reshape(blocks_here, block_rows, width)
    edges = jnp.concatenate(
        [gated_blocks[:, :EDGE], gated_blocks[:, block_rows - EDGE :]], axis=1
    )
    all_edges = lax.all_gather(edges, "seq", axis=0, tiled=True)
    before = route_row[None, :] == (own_places[:, None] - 1)
    after = route_row[None, :] == (own_places[:, None] + 1)
    low = select_blocks(before, all_edges[:, EDGE:])[:, EDGE - half :]
    high = select_blocks(after, all_edges[:, :EDGE])[:, :half]
    padded = jnp.concatenate([low, gated_blocks, high], axis=1)
    depthwise = jnp.zeros((blocks_here, block_rows, width), jnp.float32)
    for tap in range(KERNEL):
        depthwise = depthwise + depthwise_taps[tap].astype(jnp.float32)[None, None, :] * padded[
            :, tap : tap + block_rows
        ].astype(jnp.float32)
    shaped = layer_norm(depthwise.reshape(frame_rows, width), depthwise_gain)
    activated = (shaped * jax.nn.sigmoid(shaped)).astype(jnp.bfloat16)
    contracted = add_rows(activated, out_full)
    result = (after_attn.astype(jnp.float32) + contracted).astype(jnp.bfloat16)
    return result.reshape(blocks_here, block_rows, width)[None]


def solution(mesh):
    placed = (
        P("dp", "seq", None, None),
        P("dp", None),
        P("dp"),
        P(),
        P("dp", None),
        P("dp", None),
        P("dp", None),
        P("dp", None),
        P(),
        P("dp", None),
        P(),
        P(),
        P("dp", None),
    )
    return jax.shard_map(
        body, mesh=mesh, in_specs=placed, out_specs=P("dp", "seq", None, None), check_vma=False
    )
```

```python
import math

import jax
import jax.numpy as jnp
from jax import lax
from jax.sharding import PartitionSpec as P

HEAD_DIM = 64
KERNEL = 31
EDGE = 16


def layer_norm(values, gain_row):
    values = values.astype(jnp.float32)
    center = values - jnp.mean(values, axis=-1, keepdims=True)
    spread = jnp.mean(center * center, axis=-1, keepdims=True)
    return center * lax.rsqrt(spread + 1e-05) * gain_row


def select_blocks(selector, blocks):
    return jnp.einsum(
        "ab,bfc->afc", selector.astype(jnp.bfloat16), blocks, preferred_element_type=jnp.float32
    ).astype(jnp.bfloat16)


def add_rows(left, piece):
    return jnp.dot(left, piece, preferred_element_type=jnp.float32)


def body(
    frames,
    routes,
    lengths,
    attention_gain,
    query_weight,
    key_weight,
    value_weight,
    output_weight,
    convolution_gain,
    pointwise_in,
    depthwise_taps,
    depthwise_gain,
    pointwise_out,
):
    shard_index = lax.axis_index("seq")
    blocks_here = frames.shape[1]
    block_rows = frames.shape[2]
    width = frames.shape[3]
    frame_rows = blocks_here * block_rows
    route_row = routes[0]
    own_places = lax.dynamic_slice_in_dim(route_row, shard_index * blocks_here, blocks_here)
    length = lengths[0]
    ordered = frames[0].reshape(frame_rows, width)
    positions = (own_places[:, None] * block_rows + jnp.arange(block_rows)[None, :]).reshape(
        frame_rows
    )
    is_valid = positions < length
    normed = layer_norm(ordered, attention_gain).astype(jnp.bfloat16)
    att_width = query_weight.shape[1]
    qkv_local = jnp.concatenate([query_weight, key_weight, value_weight], axis=1)
    qkv_weight = lax.all_gather(qkv_local, "dp", axis=0, tiled=True)
    projected_qkv = add_rows(normed, qkv_weight).astype(jnp.bfloat16)
    head_count = att_width // HEAD_DIM
    shards = lax.axis_size("seq")
    slots = -(-head_count // shards)
    scaling = 1.0 / math.sqrt(HEAD_DIM)
    qkv_heads = projected_qkv.reshape(frame_rows, 3, head_count, HEAD_DIM)
    qkv_heads = jnp.pad(
        qkv_heads, ((0, 0), (0, 0), (0, slots * shards - head_count), (0, 0))
    ).reshape(frame_rows, 3, slots, shards, HEAD_DIM)
    outbound = qkv_heads.transpose(3, 0, 1, 2, 4)
    arrived = lax.all_to_all(outbound, "seq", split_axis=0, concat_axis=0, tiled=True)
    all_rows = shards * frame_rows
    arrived = arrived.reshape(all_rows, 3, slots, HEAD_DIM)
    query_all = arrived[:, 0]
    key_all = arrived[:, 1]
    value_all = arrived[:, 2]
    key_positions = (
        route_row[:, None] * block_rows + jnp.arange(block_rows)[None, :]
    ).reshape(all_rows)
    key_valid = key_positions < length
    pieces = []
    chunk = 4 * block_rows
    for offset in range(0, all_rows, chunk):
        stop = min(offset + chunk, all_rows)
        scores = (
            jnp.einsum(
                "qhd,khd->hqk",
                query_all[offset:stop],
                key_all,
                preferred_element_type=jnp.float32,
            )
            * scaling
        )
        scores = jnp.where(key_valid[None, None, :], scores, -1e30)
        top = jnp.max(scores, axis=2, keepdims=True)
        weights_exp = jnp.where(key_valid[None, None, :], jnp.exp(scores - top), 0.0)
        numer = jnp.einsum(
            "hqk,khd->qhd",
            weights_exp.astype(jnp.bfloat16),
            value_all,
            preferred_element_type=jnp.float32,
        )
        total = jnp.sum(weights_exp, axis=2)
        pieces.append((numer / total.T[:, :, None]).astype(jnp.bfloat16))
    mixed = jnp.concatenate(pieces, axis=0).reshape(shards, frame_rows, slots, HEAD_DIM)
    returned = lax.all_to_all(mixed, "seq", split_axis=0, concat_axis=0, tiled=True)
    attended = returned.transpose(1, 2, 0, 3).reshape(frame_rows, slots * shards * HEAD_DIM)
    attended = attended[:, :att_width]
    out_rows = output_weight.shape[0]
    in_width = pointwise_in.shape[1]
    late_local = jnp.concatenate(
        [
            output_weight.reshape(pointwise_in.shape[0], -1),
            pointwise_in,
            pointwise_out,
        ],
        axis=1,
    )
    late_weight = lax.all_gather(late_local, "dp", axis=0, tiled=True)
    out_cols = late_local.shape[1] - in_width - pointwise_out.shape[1]
    output_full = late_weight[:, :out_cols].reshape(-1, width)
    in_full = late_weight[:, out_cols : out_cols + in_width]
    out_full = late_weight[:, out_cols + in_width :]
    del out_rows
    half = KERNEL // 2
    middle = block_rows - 2 * EDGE

    def blocks_of(rows):
        return rows.reshape(blocks_here, block_rows, *rows.shape[1:])

    def edge_rows(rows):
        shaped = blocks_of(rows)
        return jnp.concatenate([shaped[:, :EDGE], shaped[:, block_rows - EDGE :]], axis=1)

    def middle_rows(rows):
        return blocks_of(rows)[:, EDGE : block_rows - EDGE]

    def frame_path(attended_rows, ordered_rows, valid_rows):
        count = attended_rows.shape[0] * attended_rows.shape[1]
        projected = add_rows(attended_rows.reshape(count, -1), output_full)
        after = (ordered_rows.reshape(count, width).astype(jnp.float32) + projected).astype(
            jnp.bfloat16
        )
        conv_normed = layer_norm(after, convolution_gain).astype(jnp.bfloat16)
        expanded = add_rows(conv_normed, in_full)
        gated = expanded[:, :width] * jax.nn.sigmoid(expanded[:, width:])
        gated = jnp.where(valid_rows.reshape(count)[:, None], gated, 0.0).astype(jnp.bfloat16)
        shape = attended_rows.shape[:2] + (width,)
        return after.reshape(shape), gated.reshape(shape)

    after_edge, edges = frame_path(edge_rows(attended), edge_rows(ordered), edge_rows(is_valid))
    all_edges = lax.all_gather(edges, "seq", axis=0, tiled=True)
    after_middle, gated_middle = frame_path(
        middle_rows(attended), middle_rows(ordered), middle_rows(is_valid)
    )
    gated_blocks = jnp.concatenate([edges[:, :EDGE], gated_middle, edges[:, EDGE:]], axis=1)
    after_blocks = jnp.concatenate(
        [after_edge[:, :EDGE], after_middle, after_edge[:, EDGE:]], axis=1
    )

    def convolve(padded, count):
        total = jnp.zeros((blocks_here, count, width), jnp.float32)
        for tap in range(KERNEL):
            total = total + depthwise_taps[tap].astype(jnp.float32)[None, None, :] * padded[
                :, tap : tap + count
            ].astype(jnp.float32)
        return total

    def finish(depthwise, after):
        count = depthwise.shape[0] * depthwise.shape[1]
        shaped = layer_norm(depthwise.reshape(count, width), depthwise_gain)
        activated = (shaped * jax.nn.sigmoid(shaped)).astype(jnp.bfloat16)
        contracted = add_rows(activated, out_full)
        result = (after.reshape(count, width).astype(jnp.float32) + contracted).astype(
            jnp.bfloat16
        )
        return result.reshape(depthwise.shape)

    inner_count = block_rows - 2 * half
    inner = finish(convolve(gated_blocks, inner_count), after_blocks[:, half : block_rows - half])
    before = route_row[None, :] == (own_places[:, None] - 1)
    after = route_row[None, :] == (own_places[:, None] + 1)
    low = select_blocks(before, all_edges[:, EDGE:])[:, EDGE - half :]
    high = select_blocks(after, all_edges[:, :EDGE])[:, :half]
    low_conv = convolve(jnp.concatenate([low, gated_blocks[:, : 2 * half]], axis=1), half)
    high_conv = convolve(
        jnp.concatenate([gated_blocks[:, block_rows - 2 * half :], high], axis=1), half
    )
    outer = finish(
        jnp.concatenate([low_conv, high_conv], axis=1),
        jnp.concatenate([after_blocks[:, :half], after_blocks[:, block_rows - half :]], axis=1),
    )
    result = jnp.concatenate([outer[:, :half], inner, outer[:, half:]], axis=1)
    del middle
    return result[None]


def solution(mesh):
    placed = (
        P("dp", "seq", None, None),
        P("dp", None),
        P("dp"),
        P(),
        P("dp", None),
        P("dp", None),
        P("dp", None),
        P("dp", None),
        P(),
        P("dp", None),
        P(),
        P(),
        P("dp", None),
    )
    return jax.shard_map(
        body, mesh=mesh, in_specs=placed, out_specs=P("dp", "seq", None, None), check_vma=False
    )
```

```python
import math

import jax
import jax.numpy as jnp
from jax import lax
from jax.experimental import pallas as pl
from jax.sharding import PartitionSpec as P

HEAD_DIM = 64
KERNEL = 31
EDGE = 16


def layer_norm(values, gain_row):
    values = values.astype(jnp.float32)
    center = values - jnp.mean(values, axis=-1, keepdims=True)
    spread = jnp.mean(center * center, axis=-1, keepdims=True)
    return center * lax.rsqrt(spread + 1e-05) * gain_row


def select_blocks(selector, blocks):
    return jnp.einsum(
        "ab,bfc->afc", selector.astype(jnp.bfloat16), blocks, preferred_element_type=jnp.float32
    ).astype(jnp.bfloat16)


def attention_kernel(mask_ref, query_ref, key_ref, value_ref, out_ref):
    scaling = 1.0 / math.sqrt(HEAD_DIM)
    scores = (
        lax.dot_general(
            query_ref[0, 0],
            key_ref[0, 0],
            (((1,), (1,)), ((), ())),
            preferred_element_type=jnp.float32,
        )
        * scaling
    )
    valid = mask_ref[...] > 0.5
    scores = jnp.where(valid, scores, -1e30)
    top = jnp.max(scores, axis=1, keepdims=True)
    weights_exp = jnp.where(valid, jnp.exp(scores - top), 0.0)
    total = jnp.sum(weights_exp, axis=1, keepdims=True)
    numer = jnp.dot(
        weights_exp.astype(jnp.bfloat16), value_ref[0, 0], preferred_element_type=jnp.float32
    )
    out_ref[0] = (numer / total).astype(out_ref.dtype)


def attend(qkv, key_valid, query_block):
    slots, rows = qkv.shape[1], qkv.shape[2]
    mask = key_valid.astype(jnp.float32)[None, :]
    return pl.pallas_call(
        attention_kernel,
        grid=(slots, rows // query_block),
        in_specs=[
            pl.BlockSpec((1, rows), lambda h, i: (0, 0)),
            pl.BlockSpec((1, 1, query_block, HEAD_DIM), lambda h, i: (0, h, i, 0)),
            pl.BlockSpec((1, 1, rows, HEAD_DIM), lambda h, i: (1, h, 0, 0)),
            pl.BlockSpec((1, 1, rows, HEAD_DIM), lambda h, i: (2, h, 0, 0)),
        ],
        out_specs=pl.BlockSpec((1, query_block, HEAD_DIM), lambda h, i: (h, i, 0)),
        out_shape=jax.ShapeDtypeStruct((slots, rows, HEAD_DIM), jnp.bfloat16),
    )(mask, qkv, qkv, qkv)


def add_rows(left, piece):
    return jnp.dot(left, piece, preferred_element_type=jnp.float32)


def body(
    frames,
    routes,
    lengths,
    attention_gain,
    query_weight,
    key_weight,
    value_weight,
    output_weight,
    convolution_gain,
    pointwise_in,
    depthwise_taps,
    depthwise_gain,
    pointwise_out,
):
    shard_index = lax.axis_index("seq")
    blocks_here = frames.shape[1]
    block_rows = frames.shape[2]
    width = frames.shape[3]
    frame_rows = blocks_here * block_rows
    route_row = routes[0]
    own_places = lax.dynamic_slice_in_dim(route_row, shard_index * blocks_here, blocks_here)
    length = lengths[0]
    ordered = frames[0].reshape(frame_rows, width)
    positions = (own_places[:, None] * block_rows + jnp.arange(block_rows)[None, :]).reshape(
        frame_rows
    )
    is_valid = positions < length
    normed = layer_norm(ordered, attention_gain).astype(jnp.bfloat16)
    att_width = query_weight.shape[1]
    qkv_local = jnp.concatenate([query_weight, key_weight, value_weight], axis=1)
    qkv_weight = lax.all_gather(qkv_local, "dp", axis=0, tiled=True)
    projected_qkv = add_rows(normed, qkv_weight).astype(jnp.bfloat16)
    head_count = att_width // HEAD_DIM
    shards = lax.axis_size("seq")
    slots = -(-head_count // shards)
    scaling = 1.0 / math.sqrt(HEAD_DIM)
    qkv_heads = projected_qkv.reshape(frame_rows, 3, head_count, HEAD_DIM)
    qkv_heads = jnp.pad(
        qkv_heads, ((0, 0), (0, 0), (0, slots * shards - head_count), (0, 0))
    ).reshape(frame_rows, 3, slots, shards, HEAD_DIM)
    outbound = qkv_heads.transpose(3, 0, 1, 2, 4)
    arrived = lax.all_to_all(outbound, "seq", split_axis=0, concat_axis=0, tiled=True)
    all_rows = shards * frame_rows
    qkv_all = arrived.transpose(2, 3, 0, 1, 4).reshape(3, slots, all_rows, HEAD_DIM)
    key_positions = (
        route_row[:, None] * block_rows + jnp.arange(block_rows)[None, :]
    ).reshape(all_rows)
    key_valid = key_positions < length
    mixed = attend(qkv_all, key_valid, 4 * block_rows)
    mixed = mixed.reshape(slots, shards, frame_rows, HEAD_DIM).transpose(1, 2, 0, 3)
    returned = lax.all_to_all(mixed, "seq", split_axis=0, concat_axis=0, tiled=True)
    attended = returned.transpose(1, 2, 0, 3).reshape(frame_rows, slots * shards * HEAD_DIM)
    attended = attended[:, :att_width]
    out_rows = output_weight.shape[0]
    in_width = pointwise_in.shape[1]
    late_local = jnp.concatenate(
        [
            output_weight.reshape(pointwise_in.shape[0], -1),
            pointwise_in,
            pointwise_out,
        ],
        axis=1,
    )
    late_weight = lax.all_gather(late_local, "dp", axis=0, tiled=True)
    out_cols = late_local.shape[1] - in_width - pointwise_out.shape[1]
    output_full = late_weight[:, :out_cols].reshape(-1, width)
    in_full = late_weight[:, out_cols : out_cols + in_width]
    out_full = late_weight[:, out_cols + in_width :]
    del out_rows
    half = KERNEL // 2
    middle = block_rows - 2 * EDGE

    def blocks_of(rows):
        return rows.reshape(blocks_here, block_rows, *rows.shape[1:])

    def edge_rows(rows):
        shaped = blocks_of(rows)
        return jnp.concatenate([shaped[:, :EDGE], shaped[:, block_rows - EDGE :]], axis=1)

    def middle_rows(rows):
        return blocks_of(rows)[:, EDGE : block_rows - EDGE]

    def frame_path(attended_rows, ordered_rows, valid_rows):
        count = attended_rows.shape[0] * attended_rows.shape[1]
        projected = add_rows(attended_rows.reshape(count, -1), output_full)
        after = (ordered_rows.reshape(count, width).astype(jnp.float32) + projected).astype(
            jnp.bfloat16
        )
        conv_normed = layer_norm(after, convolution_gain).astype(jnp.bfloat16)
        expanded = add_rows(conv_normed, in_full)
        gated = expanded[:, :width] * jax.nn.sigmoid(expanded[:, width:])
        gated = jnp.where(valid_rows.reshape(count)[:, None], gated, 0.0).astype(jnp.bfloat16)
        shape = attended_rows.shape[:2] + (width,)
        return after.reshape(shape), gated.reshape(shape)

    after_edge, edges = frame_path(edge_rows(attended), edge_rows(ordered), edge_rows(is_valid))
    all_edges = lax.all_gather(edges, "seq", axis=0, tiled=True)
    after_middle, gated_middle = frame_path(
        middle_rows(attended), middle_rows(ordered), middle_rows(is_valid)
    )
    gated_blocks = jnp.concatenate([edges[:, :EDGE], gated_middle, edges[:, EDGE:]], axis=1)
    after_blocks = jnp.concatenate(
        [after_edge[:, :EDGE], after_middle, after_edge[:, EDGE:]], axis=1
    )

    def convolve(padded, count):
        total = jnp.zeros((blocks_here, count, width), jnp.float32)
        for tap in range(KERNEL):
            total = total + depthwise_taps[tap].astype(jnp.float32)[None, None, :] * padded[
                :, tap : tap + count
            ].astype(jnp.float32)
        return total

    def finish(depthwise, after):
        count = depthwise.shape[0] * depthwise.shape[1]
        shaped = layer_norm(depthwise.reshape(count, width), depthwise_gain)
        activated = (shaped * jax.nn.sigmoid(shaped)).astype(jnp.bfloat16)
        contracted = add_rows(activated, out_full)
        result = (after.reshape(count, width).astype(jnp.float32) + contracted).astype(
            jnp.bfloat16
        )
        return result.reshape(depthwise.shape)

    inner_count = block_rows - 2 * half
    inner = finish(convolve(gated_blocks, inner_count), after_blocks[:, half : block_rows - half])
    before = route_row[None, :] == (own_places[:, None] - 1)
    after = route_row[None, :] == (own_places[:, None] + 1)
    low = select_blocks(before, all_edges[:, EDGE:])[:, EDGE - half :]
    high = select_blocks(after, all_edges[:, :EDGE])[:, :half]
    low_conv = convolve(jnp.concatenate([low, gated_blocks[:, : 2 * half]], axis=1), half)
    high_conv = convolve(
        jnp.concatenate([gated_blocks[:, block_rows - 2 * half :], high], axis=1), half
    )
    outer = finish(
        jnp.concatenate([low_conv, high_conv], axis=1),
        jnp.concatenate([after_blocks[:, :half], after_blocks[:, block_rows - half :]], axis=1),
    )
    result = jnp.concatenate([outer[:, :half], inner, outer[:, half:]], axis=1)
    del middle
    return result[None]


def solution(mesh):
    placed = (
        P("dp", "seq", None, None),
        P("dp", None),
        P("dp"),
        P(),
        P("dp", None),
        P("dp", None),
        P("dp", None),
        P("dp", None),
        P(),
        P("dp", None),
        P(),
        P(),
        P("dp", None),
    )
    return jax.shard_map(
        body, mesh=mesh, in_specs=placed, out_specs=P("dp", "seq", None, None), check_vma=False
    )
```

```python
import math

import jax
import jax.numpy as jnp
from jax import lax
from jax.experimental import pallas as pl
from jax.sharding import PartitionSpec as P

HEAD_DIM = 64
KERNEL = 31
EDGE = 16


def layer_norm(values, gain_row):
    values = values.astype(jnp.float32)
    center = values - jnp.mean(values, axis=-1, keepdims=True)
    spread = jnp.mean(center * center, axis=-1, keepdims=True)
    return center * lax.rsqrt(spread + 1e-05) * gain_row


def select_blocks(selector, blocks):
    return jnp.einsum(
        "ab,bfc->afc", selector.astype(jnp.bfloat16), blocks, preferred_element_type=jnp.float32
    ).astype(jnp.bfloat16)


def attention_kernel(mask_ref, query_ref, key_ref, value_ref, out_ref):
    scaling = 1.0 / math.sqrt(HEAD_DIM)
    scores = (
        lax.dot_general(
            query_ref[0, 0],
            key_ref[0, 0],
            (((1,), (1,)), ((), ())),
            preferred_element_type=jnp.float32,
        )
        * scaling
    )
    valid = mask_ref[...] > 0.5
    scores = jnp.where(valid, scores, -1e30)
    top = jnp.max(scores, axis=1, keepdims=True)
    weights_exp = jnp.exp(scores - top)
    total = jnp.sum(weights_exp, axis=1, keepdims=True)
    numer = jnp.dot(
        weights_exp.astype(jnp.bfloat16), value_ref[0, 0], preferred_element_type=jnp.float32
    )
    out_ref[0] = (numer / total).astype(out_ref.dtype)


def attend(qkv, key_valid, query_block):
    slots, rows = qkv.shape[1], qkv.shape[2]
    mask = key_valid.astype(jnp.float32)[None, :]
    return pl.pallas_call(
        attention_kernel,
        grid=(slots, rows // query_block),
        in_specs=[
            pl.BlockSpec((1, rows), lambda h, i: (0, 0)),
            pl.BlockSpec((1, 1, query_block, HEAD_DIM), lambda h, i: (0, h, i, 0)),
            pl.BlockSpec((1, 1, rows, HEAD_DIM), lambda h, i: (1, h, 0, 0)),
            pl.BlockSpec((1, 1, rows, HEAD_DIM), lambda h, i: (2, h, 0, 0)),
        ],
        out_specs=pl.BlockSpec((1, query_block, HEAD_DIM), lambda h, i: (h, i, 0)),
        out_shape=jax.ShapeDtypeStruct((slots, rows, HEAD_DIM), jnp.bfloat16),
    )(mask, qkv, qkv, qkv)


def add_rows(left, piece):
    return jnp.dot(left, piece, preferred_element_type=jnp.float32)


def body(
    frames,
    routes,
    lengths,
    attention_gain,
    query_weight,
    key_weight,
    value_weight,
    output_weight,
    convolution_gain,
    pointwise_in,
    depthwise_taps,
    depthwise_gain,
    pointwise_out,
):
    shard_index = lax.axis_index("seq")
    blocks_here = frames.shape[1]
    block_rows = frames.shape[2]
    width = frames.shape[3]
    frame_rows = blocks_here * block_rows
    route_row = routes[0]
    own_places = lax.dynamic_slice_in_dim(route_row, shard_index * blocks_here, blocks_here)
    length = lengths[0]
    ordered = frames[0].reshape(frame_rows, width)
    positions = (own_places[:, None] * block_rows + jnp.arange(block_rows)[None, :]).reshape(
        frame_rows
    )
    is_valid = positions < length
    normed = layer_norm(ordered, attention_gain).astype(jnp.bfloat16)
    att_width = query_weight.shape[1]
    qkv_local = jnp.concatenate([query_weight, key_weight, value_weight], axis=1)
    qkv_weight = lax.all_gather(qkv_local, "dp", axis=0, tiled=True)
    projected_qkv = add_rows(normed, qkv_weight).astype(jnp.bfloat16)
    head_count = att_width // HEAD_DIM
    shards = lax.axis_size("seq")
    slots = -(-head_count // shards)
    scaling = 1.0 / math.sqrt(HEAD_DIM)
    qkv_heads = projected_qkv.reshape(frame_rows, 3, head_count, HEAD_DIM)
    qkv_heads = jnp.pad(
        qkv_heads, ((0, 0), (0, 0), (0, slots * shards - head_count), (0, 0))
    ).reshape(frame_rows, 3, slots, shards, HEAD_DIM)
    outbound = qkv_heads.transpose(3, 0, 1, 2, 4)
    arrived = lax.all_to_all(outbound, "seq", split_axis=0, concat_axis=0, tiled=True)
    all_rows = shards * frame_rows
    qkv_all = arrived.transpose(2, 3, 0, 1, 4).reshape(3, slots, all_rows, HEAD_DIM)
    key_positions = (
        route_row[:, None] * block_rows + jnp.arange(block_rows)[None, :]
    ).reshape(all_rows)
    key_valid = key_positions < length
    mixed = attend(qkv_all, key_valid, 4 * block_rows)
    mixed = mixed.reshape(slots, shards, frame_rows, HEAD_DIM).transpose(1, 2, 0, 3)
    returned = lax.all_to_all(mixed, "seq", split_axis=0, concat_axis=0, tiled=True)
    attended = returned.transpose(1, 2, 0, 3).reshape(frame_rows, slots * shards * HEAD_DIM)
    attended = attended[:, :att_width]
    out_rows = output_weight.shape[0]
    in_width = pointwise_in.shape[1]
    late_local = jnp.concatenate(
        [
            output_weight.reshape(pointwise_in.shape[0], -1),
            pointwise_in,
            pointwise_out,
        ],
        axis=1,
    )
    late_weight = lax.all_gather(late_local, "dp", axis=0, tiled=True)
    out_cols = late_local.shape[1] - in_width - pointwise_out.shape[1]
    output_full = late_weight[:, :out_cols].reshape(-1, width)
    in_full = late_weight[:, out_cols : out_cols + in_width]
    out_full = late_weight[:, out_cols + in_width :]
    del out_rows
    half = KERNEL // 2
    middle = block_rows - 2 * EDGE

    def blocks_of(rows):
        return rows.reshape(blocks_here, block_rows, *rows.shape[1:])

    def edge_rows(rows):
        shaped = blocks_of(rows)
        return jnp.concatenate([shaped[:, :EDGE], shaped[:, block_rows - EDGE :]], axis=1)

    def middle_rows(rows):
        return blocks_of(rows)[:, EDGE : block_rows - EDGE]

    def frame_path(attended_rows, ordered_rows, valid_rows):
        count = attended_rows.shape[0] * attended_rows.shape[1]
        projected = add_rows(attended_rows.reshape(count, -1), output_full)
        after = (ordered_rows.reshape(count, width).astype(jnp.float32) + projected).astype(
            jnp.bfloat16
        )
        conv_normed = layer_norm(after, convolution_gain).astype(jnp.bfloat16)
        expanded = add_rows(conv_normed, in_full)
        gated = expanded[:, :width] * jax.nn.sigmoid(expanded[:, width:])
        gated = jnp.where(valid_rows.reshape(count)[:, None], gated, 0.0).astype(jnp.bfloat16)
        shape = attended_rows.shape[:2] + (width,)
        return after.reshape(shape), gated.reshape(shape)

    after_edge, edges = frame_path(edge_rows(attended), edge_rows(ordered), edge_rows(is_valid))
    all_edges = lax.all_gather(edges, "seq", axis=0, tiled=True)
    after_middle, gated_middle = frame_path(
        middle_rows(attended), middle_rows(ordered), middle_rows(is_valid)
    )
    gated_blocks = jnp.concatenate([edges[:, :EDGE], gated_middle, edges[:, EDGE:]], axis=1)
    after_blocks = jnp.concatenate(
        [after_edge[:, :EDGE], after_middle, after_edge[:, EDGE:]], axis=1
    )

    def convolve(padded, count):
        total = jnp.zeros((blocks_here, count, width), jnp.float32)
        for tap in range(KERNEL):
            total = total + depthwise_taps[tap].astype(jnp.float32)[None, None, :] * padded[
                :, tap : tap + count
            ].astype(jnp.float32)
        return total

    def finish(depthwise, after):
        count = depthwise.shape[0] * depthwise.shape[1]
        shaped = layer_norm(depthwise.reshape(count, width), depthwise_gain)
        activated = (shaped * jax.nn.sigmoid(shaped)).astype(jnp.bfloat16)
        contracted = add_rows(activated, out_full)
        result = (after.reshape(count, width).astype(jnp.float32) + contracted).astype(
            jnp.bfloat16
        )
        return result.reshape(depthwise.shape)

    inner = finish(
        convolve(gated_blocks[:, EDGE - half :], middle), after_blocks[:, EDGE : block_rows - EDGE]
    )
    before = route_row[None, :] == (own_places[:, None] - 1)
    after = route_row[None, :] == (own_places[:, None] + 1)
    low = select_blocks(before, all_edges[:, EDGE:])[:, EDGE - half :]
    high = select_blocks(after, all_edges[:, :EDGE])[:, :half]
    low_conv = convolve(jnp.concatenate([low, gated_blocks[:, : EDGE + half]], axis=1), EDGE)
    high_conv = convolve(
        jnp.concatenate([gated_blocks[:, block_rows - EDGE - half :], high], axis=1), EDGE
    )
    outer = finish(
        jnp.concatenate([low_conv, high_conv], axis=1),
        jnp.concatenate([after_blocks[:, :EDGE], after_blocks[:, block_rows - EDGE :]], axis=1),
    )
    result = jnp.concatenate([outer[:, :EDGE], inner, outer[:, EDGE:]], axis=1)
    del middle
    return result[None]


def solution(mesh):
    placed = (
        P("dp", "seq", None, None),
        P("dp", None),
        P("dp"),
        P(),
        P("dp", None),
        P("dp", None),
        P("dp", None),
        P("dp", None),
        P(),
        P("dp", None),
        P(),
        P(),
        P("dp", None),
    )
    return jax.shard_map(
        body, mesh=mesh, in_specs=placed, out_specs=P("dp", "seq", None, None), check_vma=False
    )
```

```python
import math

import jax
import jax.numpy as jnp
from jax import lax
from jax.experimental import pallas as pl
from jax.sharding import PartitionSpec as P

HEAD_DIM = 64
KERNEL = 31
EDGE = 16


def layer_norm(values, gain_row):
    values = values.astype(jnp.float32)
    center = values - jnp.mean(values, axis=-1, keepdims=True)
    spread = jnp.mean(center * center, axis=-1, keepdims=True)
    return center * lax.rsqrt(spread + 1e-05) * gain_row


def select_blocks(selector, blocks):
    return jnp.einsum(
        "ab,bfc->afc", selector.astype(jnp.bfloat16), blocks, preferred_element_type=jnp.float32
    ).astype(jnp.bfloat16)


def attention_kernel(mask_ref, query_ref, key_ref, value_ref, out_ref):
    scaling = 1.0 / math.sqrt(HEAD_DIM)
    sources, rows = key_ref.shape[0], key_ref.shape[3]
    keys = key_ref[:, 0, 0].reshape(sources * rows, HEAD_DIM)
    values = value_ref[:, 0, 0].reshape(sources * rows, HEAD_DIM)
    scores = (
        lax.dot_general(
            query_ref[0, 0, 0],
            keys,
            (((1,), (1,)), ((), ())),
            preferred_element_type=jnp.float32,
        )
        * scaling
    )
    valid = mask_ref[...] > 0.5
    scores = jnp.where(valid, scores, -1e30)
    top = jnp.max(scores, axis=1, keepdims=True)
    weights_exp = jnp.exp(scores - top)
    total = jnp.sum(weights_exp, axis=1, keepdims=True)
    numer = jnp.dot(weights_exp.astype(jnp.bfloat16), values, preferred_element_type=jnp.float32)
    out_ref[0, 0] = (numer / total).astype(out_ref.dtype)


def attend(qkv, key_valid):
    sources, slots, rows = qkv.shape[0], qkv.shape[2], qkv.shape[3]
    mask = key_valid.astype(jnp.float32)[None, :]
    return pl.pallas_call(
        attention_kernel,
        grid=(slots, sources),
        in_specs=[
            pl.BlockSpec((1, sources * rows), lambda h, i: (0, 0)),
            pl.BlockSpec((1, 1, 1, rows, HEAD_DIM), lambda h, i: (i, 0, h, 0, 0)),
            pl.BlockSpec((sources, 1, 1, rows, HEAD_DIM), lambda h, i: (0, 1, h, 0, 0)),
            pl.BlockSpec((sources, 1, 1, rows, HEAD_DIM), lambda h, i: (0, 2, h, 0, 0)),
        ],
        out_specs=pl.BlockSpec((1, 1, rows, HEAD_DIM), lambda h, i: (i, h, 0, 0)),
        out_shape=jax.ShapeDtypeStruct((sources, slots, rows, HEAD_DIM), jnp.bfloat16),
    )(mask, qkv, qkv, qkv)


def add_rows(left, piece):
    return jnp.dot(left, piece, preferred_element_type=jnp.float32)


def body(
    frames,
    routes,
    lengths,
    attention_gain,
    query_weight,
    key_weight,
    value_weight,
    output_weight,
    convolution_gain,
    pointwise_in,
    depthwise_taps,
    depthwise_gain,
    pointwise_out,
):
    shard_index = lax.axis_index("seq")
    blocks_here = frames.shape[1]
    block_rows = frames.shape[2]
    width = frames.shape[3]
    frame_rows = blocks_here * block_rows
    route_row = routes[0]
    own_places = lax.dynamic_slice_in_dim(route_row, shard_index * blocks_here, blocks_here)
    length = lengths[0]
    ordered = frames[0].reshape(frame_rows, width)
    positions = (own_places[:, None] * block_rows + jnp.arange(block_rows)[None, :]).reshape(
        frame_rows
    )
    is_valid = positions < length
    normed = layer_norm(ordered, attention_gain).astype(jnp.bfloat16)
    att_width = query_weight.shape[1]
    qkv_local = jnp.concatenate([query_weight, key_weight, value_weight], axis=1)
    qkv_weight = lax.all_gather(qkv_local, "dp", axis=0, tiled=True)
    projected_qkv = add_rows(normed, qkv_weight).astype(jnp.bfloat16)
    head_count = att_width // HEAD_DIM
    shards = lax.axis_size("seq")
    slots = -(-head_count // shards)
    scaling = 1.0 / math.sqrt(HEAD_DIM)
    qkv_heads = projected_qkv.reshape(frame_rows, 3, head_count, HEAD_DIM)
    qkv_heads = jnp.pad(
        qkv_heads, ((0, 0), (0, 0), (0, slots * shards - head_count), (0, 0))
    ).reshape(frame_rows, 3, slots, shards, HEAD_DIM)
    outbound = qkv_heads.transpose(3, 1, 2, 0, 4)
    arrived = lax.all_to_all(outbound, "seq", split_axis=0, concat_axis=0, tiled=True)
    all_rows = shards * frame_rows
    key_positions = (
        route_row[:, None] * block_rows + jnp.arange(block_rows)[None, :]
    ).reshape(all_rows)
    key_valid = key_positions < length
    mixed = attend(arrived, key_valid)
    returned = lax.all_to_all(mixed, "seq", split_axis=0, concat_axis=0, tiled=True)
    attended = returned.transpose(2, 1, 0, 3).reshape(frame_rows, slots * shards * HEAD_DIM)
    attended = attended[:, :att_width]
    out_rows = output_weight.shape[0]
    in_width = pointwise_in.shape[1]
    late_local = jnp.concatenate(
        [
            output_weight.reshape(pointwise_in.shape[0], -1),
            pointwise_in,
            pointwise_out,
        ],
        axis=1,
    )
    late_weight = lax.all_gather(late_local, "dp", axis=0, tiled=True)
    out_cols = late_local.shape[1] - in_width - pointwise_out.shape[1]
    output_full = late_weight[:, :out_cols].reshape(-1, width)
    in_full = late_weight[:, out_cols : out_cols + in_width]
    out_full = late_weight[:, out_cols + in_width :]
    del out_rows
    half = KERNEL // 2
    middle = block_rows - 2 * EDGE

    def blocks_of(rows):
        return rows.reshape(blocks_here, block_rows, *rows.shape[1:])

    def edge_rows(rows):
        shaped = blocks_of(rows)
        return jnp.concatenate([shaped[:, :EDGE], shaped[:, block_rows - EDGE :]], axis=1)

    def middle_rows(rows):
        return blocks_of(rows)[:, EDGE : block_rows - EDGE]

    def frame_path(attended_rows, ordered_rows, valid_rows):
        count = attended_rows.shape[0] * attended_rows.shape[1]
        projected = add_rows(attended_rows.reshape(count, -1), output_full)
        after = (ordered_rows.reshape(count, width).astype(jnp.float32) + projected).astype(
            jnp.bfloat16
        )
        conv_normed = layer_norm(after, convolution_gain).astype(jnp.bfloat16)
        expanded = add_rows(conv_normed, in_full)
        gated = expanded[:, :width] * jax.nn.sigmoid(expanded[:, width:])
        gated = jnp.where(valid_rows.reshape(count)[:, None], gated, 0.0).astype(jnp.bfloat16)
        shape = attended_rows.shape[:2] + (width,)
        return after.reshape(shape), gated.reshape(shape)

    after_edge, edges = frame_path(edge_rows(attended), edge_rows(ordered), edge_rows(is_valid))
    all_edges = lax.all_gather(edges, "seq", axis=0, tiled=True)
    after_middle, gated_middle = frame_path(
        middle_rows(attended), middle_rows(ordered), middle_rows(is_valid)
    )
    gated_blocks = jnp.concatenate([edges[:, :EDGE], gated_middle, edges[:, EDGE:]], axis=1)
    after_blocks = jnp.concatenate(
        [after_edge[:, :EDGE], after_middle, after_edge[:, EDGE:]], axis=1
    )

    def convolve(padded, count):
        total = jnp.zeros((blocks_here, count, width), jnp.float32)
        for tap in range(KERNEL):
            total = total + depthwise_taps[tap].astype(jnp.float32)[None, None, :] * padded[
                :, tap : tap + count
            ].astype(jnp.float32)
        return total

    def finish(depthwise, after):
        count = depthwise.shape[0] * depthwise.shape[1]
        shaped = layer_norm(depthwise.reshape(count, width), depthwise_gain)
        activated = (shaped * jax.nn.sigmoid(shaped)).astype(jnp.bfloat16)
        contracted = add_rows(activated, out_full)
        result = (after.reshape(count, width).astype(jnp.float32) + contracted).astype(
            jnp.bfloat16
        )
        return result.reshape(depthwise.shape)

    inner = finish(
        convolve(gated_blocks[:, EDGE - half :], middle), after_blocks[:, EDGE : block_rows - EDGE]
    )
    before = route_row[None, :] == (own_places[:, None] - 1)
    after = route_row[None, :] == (own_places[:, None] + 1)
    low = select_blocks(before, all_edges[:, EDGE:])[:, EDGE - half :]
    high = select_blocks(after, all_edges[:, :EDGE])[:, :half]
    low_conv = convolve(jnp.concatenate([low, gated_blocks[:, : EDGE + half]], axis=1), EDGE)
    high_conv = convolve(
        jnp.concatenate([gated_blocks[:, block_rows - EDGE - half :], high], axis=1), EDGE
    )
    outer = finish(
        jnp.concatenate([low_conv, high_conv], axis=1),
        jnp.concatenate([after_blocks[:, :EDGE], after_blocks[:, block_rows - EDGE :]], axis=1),
    )
    result = jnp.concatenate([outer[:, :EDGE], inner, outer[:, EDGE:]], axis=1)
    del middle
    return result[None]


def solution(mesh):
    placed = (
        P("dp", "seq", None, None),
        P("dp", None),
        P("dp"),
        P(),
        P("dp", None),
        P("dp", None),
        P("dp", None),
        P("dp", None),
        P(),
        P("dp", None),
        P(),
        P(),
        P("dp", None),
    )
    return jax.shard_map(
        body, mesh=mesh, in_specs=placed, out_specs=P("dp", "seq", None, None), check_vma=False
    )
```

```python
import math

import jax
import jax.numpy as jnp
from jax import lax
from jax.experimental import pallas as pl
from jax.sharding import PartitionSpec as P

HEAD_DIM = 64
KERNEL = 31
EDGE = 16


def layer_norm(values, gain_row):
    values = values.astype(jnp.float32)
    center = values - jnp.mean(values, axis=-1, keepdims=True)
    spread = jnp.mean(center * center, axis=-1, keepdims=True)
    return center * lax.rsqrt(spread + 1e-05) * gain_row


def select_blocks(selector, blocks):
    return jnp.einsum(
        "ab,bfc->afc", selector.astype(jnp.bfloat16), blocks, preferred_element_type=jnp.float32
    ).astype(jnp.bfloat16)


def attention_kernel(mask_ref, query_ref, key_ref, value_ref, out_ref):
    scaling = 1.0 / math.sqrt(HEAD_DIM)
    sources, rows = key_ref.shape[0], key_ref.shape[4]
    query_t = query_ref[0, 0, 0]
    scores = jnp.concatenate(
        [
            lax.dot_general(
                key_ref[source, 0, 0],
                query_t,
                (((0,), (0,)), ((), ())),
                preferred_element_type=jnp.float32,
            )
            for source in range(sources)
        ],
        axis=0,
    ) * scaling
    valid = mask_ref[...] > 0.5
    scores = jnp.where(valid, scores, -1e30)
    top = jnp.max(scores, axis=0, keepdims=True)
    weights_exp = jnp.exp(scores - top)
    total = jnp.sum(weights_exp, axis=0, keepdims=True)
    weights_low = weights_exp.astype(jnp.bfloat16)
    numer = jnp.zeros((HEAD_DIM, rows), jnp.float32)
    for source in range(sources):
        numer = numer + jnp.dot(
            value_ref[source, 0, 0],
            weights_low[source * rows : (source + 1) * rows],
            preferred_element_type=jnp.float32,
        )
    out_ref[0, 0] = (numer / total).astype(out_ref.dtype)


def attend(qkv, key_valid):
    sources, slots, rows = qkv.shape[0], qkv.shape[2], qkv.shape[4]
    mask = key_valid.astype(jnp.float32)[:, None]
    return pl.pallas_call(
        attention_kernel,
        grid=(slots, sources),
        in_specs=[
            pl.BlockSpec((sources * rows, 1), lambda h, i: (0, 0)),
            pl.BlockSpec((1, 1, 1, HEAD_DIM, rows), lambda h, i: (i, 0, h, 0, 0)),
            pl.BlockSpec((sources, 1, 1, HEAD_DIM, rows), lambda h, i: (0, 1, h, 0, 0)),
            pl.BlockSpec((sources, 1, 1, HEAD_DIM, rows), lambda h, i: (0, 2, h, 0, 0)),
        ],
        out_specs=pl.BlockSpec((1, 1, HEAD_DIM, rows), lambda h, i: (i, h, 0, 0)),
        out_shape=jax.ShapeDtypeStruct((sources, slots, HEAD_DIM, rows), jnp.bfloat16),
    )(mask, qkv, qkv, qkv)


def add_rows(left, piece):
    return jnp.dot(left, piece, preferred_element_type=jnp.float32)


def body(
    frames,
    routes,
    lengths,
    attention_gain,
    query_weight,
    key_weight,
    value_weight,
    output_weight,
    convolution_gain,
    pointwise_in,
    depthwise_taps,
    depthwise_gain,
    pointwise_out,
):
    shard_index = lax.axis_index("seq")
    blocks_here = frames.shape[1]
    block_rows = frames.shape[2]
    width = frames.shape[3]
    frame_rows = blocks_here * block_rows
    route_row = routes[0]
    own_places = lax.dynamic_slice_in_dim(route_row, shard_index * blocks_here, blocks_here)
    length = lengths[0]
    ordered = frames[0].reshape(frame_rows, width)
    positions = (own_places[:, None] * block_rows + jnp.arange(block_rows)[None, :]).reshape(
        frame_rows
    )
    is_valid = positions < length
    normed = layer_norm(ordered, attention_gain).astype(jnp.bfloat16)
    att_width = query_weight.shape[1]
    head_count = att_width // HEAD_DIM
    shards = lax.axis_size("seq")
    slots = -(-head_count // shards)
    blank = jnp.zeros((query_weight.shape[0], HEAD_DIM), query_weight.dtype)
    columns = []
    for target in range(shards):
        for kind in (query_weight, key_weight, value_weight):
            for slot in range(slots):
                head = slot * shards + target
                if head < head_count:
                    columns.append(kind[:, head * HEAD_DIM : (head + 1) * HEAD_DIM])
                else:
                    columns.append(blank)
    qkv_local = jnp.concatenate(columns, axis=1)
    qkv_weight = lax.all_gather(qkv_local, "dp", axis=0, tiled=True)
    projected_t = lax.dot_general(
        qkv_weight, normed, (((0,), (1,)), ((), ())), preferred_element_type=jnp.float32
    ).astype(jnp.bfloat16)
    outbound = projected_t.reshape(shards, 3, slots, HEAD_DIM, frame_rows)
    arrived = lax.all_to_all(outbound, "seq", split_axis=0, concat_axis=0, tiled=True)
    all_rows = shards * frame_rows
    key_positions = (
        route_row[:, None] * block_rows + jnp.arange(block_rows)[None, :]
    ).reshape(all_rows)
    key_valid = key_positions < length
    mixed = attend(arrived, key_valid)
    returned = lax.all_to_all(mixed, "seq", split_axis=0, concat_axis=0, tiled=True)
    attended = returned.transpose(3, 1, 0, 2).reshape(frame_rows, slots * shards * HEAD_DIM)
    attended = attended[:, :att_width]
    out_rows = output_weight.shape[0]
    in_width = pointwise_in.shape[1]
    late_local = jnp.concatenate(
        [
            output_weight.reshape(pointwise_in.shape[0], -1),
            pointwise_in,
            pointwise_out,
        ],
        axis=1,
    )
    late_weight = lax.all_gather(late_local, "dp", axis=0, tiled=True)
    out_cols = late_local.shape[1] - in_width - pointwise_out.shape[1]
    output_full = late_weight[:, :out_cols].reshape(-1, width)
    in_full = late_weight[:, out_cols : out_cols + in_width]
    out_full = late_weight[:, out_cols + in_width :]
    del out_rows
    half = KERNEL // 2
    middle = block_rows - 2 * EDGE

    def blocks_of(rows):
        return rows.reshape(blocks_here, block_rows, *rows.shape[1:])

    def edge_rows(rows):
        shaped = blocks_of(rows)
        return jnp.concatenate([shaped[:, :EDGE], shaped[:, block_rows - EDGE :]], axis=1)

    def middle_rows(rows):
        return blocks_of(rows)[:, EDGE : block_rows - EDGE]

    def frame_path(attended_rows, ordered_rows, valid_rows):
        count = attended_rows.shape[0] * attended_rows.shape[1]
        projected = add_rows(attended_rows.reshape(count, -1), output_full)
        after = (ordered_rows.reshape(count, width).astype(jnp.float32) + projected).astype(
            jnp.bfloat16
        )
        conv_normed = layer_norm(after, convolution_gain).astype(jnp.bfloat16)
        expanded = add_rows(conv_normed, in_full)
        gated = expanded[:, :width] * jax.nn.sigmoid(expanded[:, width:])
        gated = jnp.where(valid_rows.reshape(count)[:, None], gated, 0.0).astype(jnp.bfloat16)
        shape = attended_rows.shape[:2] + (width,)
        return after.reshape(shape), gated.reshape(shape)

    after_edge, edges = frame_path(edge_rows(attended), edge_rows(ordered), edge_rows(is_valid))
    all_edges = lax.all_gather(edges, "seq", axis=0, tiled=True)
    after_middle, gated_middle = frame_path(
        middle_rows(attended), middle_rows(ordered), middle_rows(is_valid)
    )
    gated_blocks = jnp.concatenate([edges[:, :EDGE], gated_middle, edges[:, EDGE:]], axis=1)
    after_blocks = jnp.concatenate(
        [after_edge[:, :EDGE], after_middle, after_edge[:, EDGE:]], axis=1
    )

    def convolve(padded, count):
        total = jnp.zeros((blocks_here, count, width), jnp.float32)
        for tap in range(KERNEL):
            total = total + depthwise_taps[tap].astype(jnp.float32)[None, None, :] * padded[
                :, tap : tap + count
            ].astype(jnp.float32)
        return total

    def finish(depthwise, after):
        count = depthwise.shape[0] * depthwise.shape[1]
        shaped = layer_norm(depthwise.reshape(count, width), depthwise_gain)
        activated = (shaped * jax.nn.sigmoid(shaped)).astype(jnp.bfloat16)
        contracted = add_rows(activated, out_full)
        result = (after.reshape(count, width).astype(jnp.float32) + contracted).astype(
            jnp.bfloat16
        )
        return result.reshape(depthwise.shape)

    inner = finish(
        convolve(gated_blocks[:, EDGE - half :], middle), after_blocks[:, EDGE : block_rows - EDGE]
    )
    before = route_row[None, :] == (own_places[:, None] - 1)
    after = route_row[None, :] == (own_places[:, None] + 1)
    low = select_blocks(before, all_edges[:, EDGE:])[:, EDGE - half :]
    high = select_blocks(after, all_edges[:, :EDGE])[:, :half]
    low_conv = convolve(jnp.concatenate([low, gated_blocks[:, : EDGE + half]], axis=1), EDGE)
    high_conv = convolve(
        jnp.concatenate([gated_blocks[:, block_rows - EDGE - half :], high], axis=1), EDGE
    )
    outer = finish(
        jnp.concatenate([low_conv, high_conv], axis=1),
        jnp.concatenate([after_blocks[:, :EDGE], after_blocks[:, block_rows - EDGE :]], axis=1),
    )
    result = jnp.concatenate([outer[:, :EDGE], inner, outer[:, EDGE:]], axis=1)
    del middle
    return result[None]


def solution(mesh):
    placed = (
        P("dp", "seq", None, None),
        P("dp", None),
        P("dp"),
        P(),
        P("dp", None),
        P("dp", None),
        P("dp", None),
        P("dp", None),
        P(),
        P("dp", None),
        P(),
        P(),
        P("dp", None),
    )
    return jax.shard_map(
        body, mesh=mesh, in_specs=placed, out_specs=P("dp", "seq", None, None), check_vma=False
    )
```

```python
import math

import jax
import jax.numpy as jnp
from jax import lax
from jax.experimental import pallas as pl
from jax.sharding import PartitionSpec as P

HEAD_DIM = 64
KERNEL = 31
EDGE = 16


def layer_norm(values, gain_row):
    values = values.astype(jnp.float32)
    center = values - jnp.mean(values, axis=-1, keepdims=True)
    spread = jnp.mean(center * center, axis=-1, keepdims=True)
    return center * lax.rsqrt(spread + 1e-05) * gain_row


def select_blocks(selector, blocks):
    return jnp.einsum(
        "ab,bfc->afc", selector.astype(jnp.bfloat16), blocks, preferred_element_type=jnp.float32
    ).astype(jnp.bfloat16)


def attention_kernel(mask_ref, query_ref, key_ref, value_ref, out_ref):
    scaling = 1.0 / math.sqrt(HEAD_DIM)
    sources, rows = key_ref.shape[0], key_ref.shape[4]
    query_t = query_ref[0, 0, 0]
    scores = jnp.concatenate(
        [
            lax.dot_general(
                key_ref[source, 0, 0],
                query_t,
                (((0,), (0,)), ((), ())),
                preferred_element_type=jnp.float32,
            )
            for source in range(sources)
        ],
        axis=0,
    ) * scaling
    valid = mask_ref[...] > 0.5
    scores = jnp.where(valid, scores, -1e30)
    top = jnp.max(scores, axis=0, keepdims=True)
    weights_exp = jnp.exp(scores - top)
    total = jnp.sum(weights_exp, axis=0, keepdims=True)
    weights_low = weights_exp.astype(jnp.bfloat16)
    numer = jnp.zeros((HEAD_DIM, rows), jnp.float32)
    for source in range(sources):
        numer = numer + jnp.dot(
            value_ref[source, 0, 0],
            weights_low[source * rows : (source + 1) * rows],
            preferred_element_type=jnp.float32,
        )
    out_ref[0, 0] = (numer / total).astype(out_ref.dtype)


def attend(qkv, key_valid):
    sources, slots, rows = qkv.shape[0], qkv.shape[2], qkv.shape[4]
    mask = key_valid.astype(jnp.float32)[:, None]
    return pl.pallas_call(
        attention_kernel,
        grid=(slots, sources),
        in_specs=[
            pl.BlockSpec((sources * rows, 1), lambda h, i: (0, 0)),
            pl.BlockSpec((1, 1, 1, HEAD_DIM, rows), lambda h, i: (i, 0, h, 0, 0)),
            pl.BlockSpec((sources, 1, 1, HEAD_DIM, rows), lambda h, i: (0, 1, h, 0, 0)),
            pl.BlockSpec((sources, 1, 1, HEAD_DIM, rows), lambda h, i: (0, 2, h, 0, 0)),
        ],
        out_specs=pl.BlockSpec((1, 1, HEAD_DIM, rows), lambda h, i: (i, h, 0, 0)),
        out_shape=jax.ShapeDtypeStruct((sources, slots, HEAD_DIM, rows), jnp.bfloat16),
    )(mask, qkv, qkv, qkv)


def add_rows(left, piece):
    return jnp.dot(left, piece, preferred_element_type=jnp.float32)


def body(
    frames,
    routes,
    lengths,
    attention_gain,
    query_weight,
    key_weight,
    value_weight,
    output_weight,
    convolution_gain,
    pointwise_in,
    depthwise_taps,
    depthwise_gain,
    pointwise_out,
):
    shard_index = lax.axis_index("seq")
    blocks_here = frames.shape[1]
    block_rows = frames.shape[2]
    width = frames.shape[3]
    frame_rows = blocks_here * block_rows
    route_row = routes[0]
    own_places = lax.dynamic_slice_in_dim(route_row, shard_index * blocks_here, blocks_here)
    length = lengths[0]
    ordered = frames[0].reshape(frame_rows, width)
    positions = (own_places[:, None] * block_rows + jnp.arange(block_rows)[None, :]).reshape(
        frame_rows
    )
    is_valid = positions < length
    normed = layer_norm(ordered, attention_gain).astype(jnp.bfloat16)
    att_width = query_weight.shape[1]
    head_count = att_width // HEAD_DIM
    shards = lax.axis_size("seq")
    slots = -(-head_count // shards)
    qkv_local = jnp.concatenate([query_weight, key_weight, value_weight], axis=1)
    qkv_weight = lax.all_gather(qkv_local, "dp", axis=0, tiled=True)
    projected_t = lax.dot_general(
        qkv_weight, normed, (((0,), (1,)), ((), ())), preferred_element_type=jnp.float32
    ).astype(jnp.bfloat16)
    projected_t = projected_t.reshape(3, head_count, HEAD_DIM, frame_rows)
    projected_t = jnp.pad(
        projected_t, ((0, 0), (0, slots * shards - head_count), (0, 0), (0, 0))
    ).reshape(3, slots, shards, HEAD_DIM, frame_rows)
    outbound = projected_t.transpose(2, 0, 1, 3, 4)
    arrived = lax.all_to_all(outbound, "seq", split_axis=0, concat_axis=0, tiled=True)
    all_rows = shards * frame_rows
    key_positions = (
        route_row[:, None] * block_rows + jnp.arange(block_rows)[None, :]
    ).reshape(all_rows)
    key_valid = key_positions < length
    mixed = attend(arrived, key_valid)
    returned = lax.all_to_all(mixed, "seq", split_axis=0, concat_axis=0, tiled=True)
    attended = returned.transpose(3, 1, 0, 2).reshape(frame_rows, slots * shards * HEAD_DIM)
    attended = attended[:, :att_width]
    out_rows = output_weight.shape[0]
    in_width = pointwise_in.shape[1]
    late_local = jnp.concatenate(
        [
            output_weight.reshape(pointwise_in.shape[0], -1),
            pointwise_in,
            pointwise_out,
        ],
        axis=1,
    )
    late_weight = lax.all_gather(late_local, "dp", axis=0, tiled=True)
    out_cols = late_local.shape[1] - in_width - pointwise_out.shape[1]
    output_full = late_weight[:, :out_cols].reshape(-1, width)
    in_full = late_weight[:, out_cols : out_cols + in_width]
    out_full = late_weight[:, out_cols + in_width :]
    del out_rows
    half = KERNEL // 2
    middle = block_rows - 2 * EDGE

    def blocks_of(rows):
        return rows.reshape(blocks_here, block_rows, *rows.shape[1:])

    def edge_rows(rows):
        shaped = blocks_of(rows)
        return jnp.concatenate([shaped[:, :EDGE], shaped[:, block_rows - EDGE :]], axis=1)

    def middle_rows(rows):
        return blocks_of(rows)[:, EDGE : block_rows - EDGE]

    def frame_path(attended_rows, ordered_rows, valid_rows):
        count = attended_rows.shape[0] * attended_rows.shape[1]
        projected = add_rows(attended_rows.reshape(count, -1), output_full)
        after = (ordered_rows.reshape(count, width).astype(jnp.float32) + projected).astype(
            jnp.bfloat16
        )
        conv_normed = layer_norm(after, convolution_gain).astype(jnp.bfloat16)
        expanded = add_rows(conv_normed, in_full)
        gated = expanded[:, :width] * jax.nn.sigmoid(expanded[:, width:])
        gated = jnp.where(valid_rows.reshape(count)[:, None], gated, 0.0).astype(jnp.bfloat16)
        shape = attended_rows.shape[:2] + (width,)
        return after.reshape(shape), gated.reshape(shape)

    after_edge, edges = frame_path(edge_rows(attended), edge_rows(ordered), edge_rows(is_valid))
    all_edges = lax.all_gather(edges, "seq", axis=0, tiled=True)
    after_middle, gated_middle = frame_path(
        middle_rows(attended), middle_rows(ordered), middle_rows(is_valid)
    )
    gated_blocks = jnp.concatenate([edges[:, :EDGE], gated_middle, edges[:, EDGE:]], axis=1)
    after_blocks = jnp.concatenate(
        [after_edge[:, :EDGE], after_middle, after_edge[:, EDGE:]], axis=1
    )

    def convolve(padded, count):
        total = jnp.zeros((blocks_here, count, width), jnp.float32)
        for tap in range(KERNEL):
            total = total + depthwise_taps[tap].astype(jnp.float32)[None, None, :] * padded[
                :, tap : tap + count
            ].astype(jnp.float32)
        return total

    def finish(depthwise, after):
        count = depthwise.shape[0] * depthwise.shape[1]
        shaped = layer_norm(depthwise.reshape(count, width), depthwise_gain)
        activated = (shaped * jax.nn.sigmoid(shaped)).astype(jnp.bfloat16)
        contracted = add_rows(activated, out_full)
        result = (after.reshape(count, width).astype(jnp.float32) + contracted).astype(
            jnp.bfloat16
        )
        return result.reshape(depthwise.shape)

    inner = finish(
        convolve(gated_blocks[:, EDGE - half :], middle), after_blocks[:, EDGE : block_rows - EDGE]
    )
    before = route_row[None, :] == (own_places[:, None] - 1)
    after = route_row[None, :] == (own_places[:, None] + 1)
    low = select_blocks(before, all_edges[:, EDGE:])[:, EDGE - half :]
    high = select_blocks(after, all_edges[:, :EDGE])[:, :half]
    low_conv = convolve(jnp.concatenate([low, gated_blocks[:, : EDGE + half]], axis=1), EDGE)
    high_conv = convolve(
        jnp.concatenate([gated_blocks[:, block_rows - EDGE - half :], high], axis=1), EDGE
    )
    outer = finish(
        jnp.concatenate([low_conv, high_conv], axis=1),
        jnp.concatenate([after_blocks[:, :EDGE], after_blocks[:, block_rows - EDGE :]], axis=1),
    )
    result = jnp.concatenate([outer[:, :EDGE], inner, outer[:, EDGE:]], axis=1)
    del middle
    return result[None]


def solution(mesh):
    placed = (
        P("dp", "seq", None, None),
        P("dp", None),
        P("dp"),
        P(),
        P("dp", None),
        P("dp", None),
        P("dp", None),
        P("dp", None),
        P(),
        P("dp", None),
        P(),
        P(),
        P("dp", None),
    )
    return jax.shard_map(
        body, mesh=mesh, in_specs=placed, out_specs=P("dp", "seq", None, None), check_vma=False
    )
```

```python
import math

import jax
import jax.numpy as jnp
from jax import lax
from jax.experimental import pallas as pl
from jax.sharding import PartitionSpec as P

HEAD_DIM = 64
KERNEL = 31
EDGE = 16


def layer_norm(values, gain_row):
    values = values.astype(jnp.float32)
    center = values - jnp.mean(values, axis=-1, keepdims=True)
    spread = jnp.mean(center * center, axis=-1, keepdims=True)
    return center * lax.rsqrt(spread + 1e-05) * gain_row


def select_blocks(selector, blocks):
    return jnp.einsum(
        "ab,bfc->afc", selector.astype(jnp.bfloat16), blocks, preferred_element_type=jnp.float32
    ).astype(jnp.bfloat16)


def attention_kernel(mask_ref, query_ref, key_ref, value_ref, out_ref):
    scaling = 1.0 / math.sqrt(HEAD_DIM)
    sources, rows = key_ref.shape[0], key_ref.shape[4]
    query_t = query_ref[0, 0, 0]
    scores = jnp.concatenate(
        [
            lax.dot_general(
                key_ref[source, 0, 0],
                query_t,
                (((0,), (0,)), ((), ())),
                preferred_element_type=jnp.float32,
            )
            for source in range(sources)
        ],
        axis=0,
    ) * scaling
    valid = mask_ref[...] > 0.5
    scores = jnp.where(valid, scores, -1e30)
    top = jnp.max(scores, axis=0, keepdims=True)
    weights_exp = jnp.exp(scores - top)
    total = jnp.sum(weights_exp, axis=0, keepdims=True)
    weights_low = weights_exp.astype(jnp.bfloat16)
    numer = jnp.zeros((HEAD_DIM, rows), jnp.float32)
    for source in range(sources):
        numer = numer + jnp.dot(
            value_ref[source, 0, 0],
            weights_low[source * rows : (source + 1) * rows],
            preferred_element_type=jnp.float32,
        )
    out_ref[0, 0] = (numer / total).astype(out_ref.dtype)


def attend(qkv, key_valid):
    sources, slots, rows = qkv.shape[0], qkv.shape[2], qkv.shape[4]
    mask = key_valid.astype(jnp.float32)[:, None]
    return pl.pallas_call(
        attention_kernel,
        grid=(slots, sources),
        in_specs=[
            pl.BlockSpec((sources * rows, 1), lambda h, i: (0, 0)),
            pl.BlockSpec((1, 1, 1, HEAD_DIM, rows), lambda h, i: (i, 0, h, 0, 0)),
            pl.BlockSpec((sources, 1, 1, HEAD_DIM, rows), lambda h, i: (0, 1, h, 0, 0)),
            pl.BlockSpec((sources, 1, 1, HEAD_DIM, rows), lambda h, i: (0, 2, h, 0, 0)),
        ],
        out_specs=pl.BlockSpec((1, 1, HEAD_DIM, rows), lambda h, i: (i, h, 0, 0)),
        out_shape=jax.ShapeDtypeStruct((sources, slots, HEAD_DIM, rows), jnp.bfloat16),
    )(mask, qkv, qkv, qkv)


def add_rows(left, piece):
    return jnp.dot(left, piece, preferred_element_type=jnp.float32)


def body(
    frames,
    routes,
    lengths,
    attention_gain,
    query_weight,
    key_weight,
    value_weight,
    output_weight,
    convolution_gain,
    pointwise_in,
    depthwise_taps,
    depthwise_gain,
    pointwise_out,
):
    shard_index = lax.axis_index("seq")
    blocks_here = frames.shape[1]
    block_rows = frames.shape[2]
    width = frames.shape[3]
    frame_rows = blocks_here * block_rows
    route_row = routes[0]
    own_places = lax.dynamic_slice_in_dim(route_row, shard_index * blocks_here, blocks_here)
    length = lengths[0]
    ordered = frames[0].reshape(frame_rows, width)
    positions = (own_places[:, None] * block_rows + jnp.arange(block_rows)[None, :]).reshape(
        frame_rows
    )
    is_valid = positions < length
    normed = layer_norm(ordered, attention_gain).astype(jnp.bfloat16)
    att_width = query_weight.shape[1]
    head_count = att_width // HEAD_DIM
    shards = lax.axis_size("seq")
    slots = -(-head_count // shards)
    qkv_local = jnp.concatenate([query_weight, key_weight, value_weight], axis=1)
    qkv_weight = lax.all_gather(qkv_local, "dp", axis=0, tiled=True)
    projected_t = lax.dot_general(
        qkv_weight, normed, (((0,), (1,)), ((), ())), preferred_element_type=jnp.float32
    ).astype(jnp.bfloat16)
    projected_t = projected_t.reshape(3, head_count, HEAD_DIM, frame_rows)
    projected_t = jnp.pad(
        projected_t, ((0, 0), (0, slots * shards - head_count), (0, 0), (0, 0))
    ).reshape(3, slots, shards, HEAD_DIM, frame_rows)
    outbound = projected_t.transpose(2, 0, 1, 3, 4)
    arrived = lax.all_to_all(outbound, "seq", split_axis=0, concat_axis=0, tiled=True)
    all_rows = shards * frame_rows
    key_positions = (
        route_row[:, None] * block_rows + jnp.arange(block_rows)[None, :]
    ).reshape(all_rows)
    key_valid = key_positions < length
    mixed = attend(arrived, key_valid)
    returned = lax.all_to_all(mixed, "seq", split_axis=0, concat_axis=0, tiled=True)
    attended = returned.transpose(3, 1, 0, 2).reshape(frame_rows, slots * shards * HEAD_DIM)
    attended = attended[:, :att_width]
    out_rows = output_weight.shape[0]
    in_width = pointwise_in.shape[1]
    late_local = jnp.concatenate(
        [
            jnp.concatenate(
                [output_weight[:, : width // 2], output_weight[:, width // 2 :]], axis=0
            ),
            pointwise_in,
            pointwise_out,
        ],
        axis=1,
    )
    late_weight = lax.all_gather(late_local, "dp", axis=0, tiled=True)
    out_cols = late_local.shape[1] - in_width - pointwise_out.shape[1]
    output_halves = late_weight[:, :out_cols].reshape(
        -1, 2, output_weight.shape[0], out_cols
    )
    output_parts = [
        output_halves[:, half].reshape(-1, out_cols) for half in range(2)
    ]
    in_full = late_weight[:, out_cols : out_cols + in_width]
    out_full = late_weight[:, out_cols + in_width :]
    del out_rows
    half = KERNEL // 2
    middle = block_rows - 2 * EDGE

    def blocks_of(rows):
        return rows.reshape(blocks_here, block_rows, *rows.shape[1:])

    def edge_rows(rows):
        shaped = blocks_of(rows)
        return jnp.concatenate([shaped[:, :EDGE], shaped[:, block_rows - EDGE :]], axis=1)

    def middle_rows(rows):
        return blocks_of(rows)[:, EDGE : block_rows - EDGE]

    def frame_path(attended_rows, ordered_rows, valid_rows):
        count = attended_rows.shape[0] * attended_rows.shape[1]
        flat = attended_rows.reshape(count, -1)
        projected = jnp.concatenate([add_rows(flat, part) for part in output_parts], axis=1)
        after = (ordered_rows.reshape(count, width).astype(jnp.float32) + projected).astype(
            jnp.bfloat16
        )
        conv_normed = layer_norm(after, convolution_gain).astype(jnp.bfloat16)
        expanded = add_rows(conv_normed, in_full)
        gated = expanded[:, :width] * jax.nn.sigmoid(expanded[:, width:])
        gated = jnp.where(valid_rows.reshape(count)[:, None], gated, 0.0).astype(jnp.bfloat16)
        shape = attended_rows.shape[:2] + (width,)
        return after.reshape(shape), gated.reshape(shape)

    after_edge, edges = frame_path(edge_rows(attended), edge_rows(ordered), edge_rows(is_valid))
    all_edges = lax.all_gather(edges, "seq", axis=0, tiled=True)
    after_middle, gated_middle = frame_path(
        middle_rows(attended), middle_rows(ordered), middle_rows(is_valid)
    )
    gated_blocks = jnp.concatenate([edges[:, :EDGE], gated_middle, edges[:, EDGE:]], axis=1)
    after_blocks = jnp.concatenate(
        [after_edge[:, :EDGE], after_middle, after_edge[:, EDGE:]], axis=1
    )

    def convolve(padded, count):
        total = jnp.zeros((blocks_here, count, width), jnp.float32)
        for tap in range(KERNEL):
            total = total + depthwise_taps[tap].astype(jnp.float32)[None, None, :] * padded[
                :, tap : tap + count
            ].astype(jnp.float32)
        return total

    def finish(depthwise, after):
        count = depthwise.shape[0] * depthwise.shape[1]
        shaped = layer_norm(depthwise.reshape(count, width), depthwise_gain)
        activated = (shaped * jax.nn.sigmoid(shaped)).astype(jnp.bfloat16)
        contracted = add_rows(activated, out_full)
        result = (after.reshape(count, width).astype(jnp.float32) + contracted).astype(
            jnp.bfloat16
        )
        return result.reshape(depthwise.shape)

    inner = finish(
        convolve(gated_blocks[:, EDGE - half :], middle), after_blocks[:, EDGE : block_rows - EDGE]
    )
    before = route_row[None, :] == (own_places[:, None] - 1)
    after = route_row[None, :] == (own_places[:, None] + 1)
    low = select_blocks(before, all_edges[:, EDGE:])[:, EDGE - half :]
    high = select_blocks(after, all_edges[:, :EDGE])[:, :half]
    low_conv = convolve(jnp.concatenate([low, gated_blocks[:, : EDGE + half]], axis=1), EDGE)
    high_conv = convolve(
        jnp.concatenate([gated_blocks[:, block_rows - EDGE - half :], high], axis=1), EDGE
    )
    outer = finish(
        jnp.concatenate([low_conv, high_conv], axis=1),
        jnp.concatenate([after_blocks[:, :EDGE], after_blocks[:, block_rows - EDGE :]], axis=1),
    )
    result = jnp.concatenate([outer[:, :EDGE], inner, outer[:, EDGE:]], axis=1)
    del middle
    return result[None]


def solution(mesh):
    placed = (
        P("dp", "seq", None, None),
        P("dp", None),
        P("dp"),
        P(),
        P("dp", None),
        P("dp", None),
        P("dp", None),
        P("dp", None),
        P(),
        P("dp", None),
        P(),
        P(),
        P("dp", None),
    )
    return jax.shard_map(
        body, mesh=mesh, in_specs=placed, out_specs=P("dp", "seq", None, None), check_vma=False
    )
```

```python
import functools
import math

import jax
import jax.numpy as jnp
from jax import lax
from jax.experimental import pallas as pl
from jax.experimental.pallas import tpu as pltpu
from jax.sharding import PartitionSpec as P

HEAD_DIM = 64
KERNEL = 31
EDGE = 16


def layer_norm(values, gain_row):
    values = values.astype(jnp.float32)
    center = values - jnp.mean(values, axis=-1, keepdims=True)
    spread = jnp.mean(center * center, axis=-1, keepdims=True)
    return center * lax.rsqrt(spread + 1e-05) * gain_row


def select_blocks(selector, blocks):
    return jnp.einsum(
        "ab,bfc->afc", selector.astype(jnp.bfloat16), blocks, preferred_element_type=jnp.float32
    ).astype(jnp.bfloat16)


def attention_kernel(mask_ref, query_ref, key_ref, value_ref, out_ref):
    scaling = 1.0 / math.sqrt(HEAD_DIM)
    sources, rows = key_ref.shape[0], key_ref.shape[4]
    query_t = query_ref[0, 0, 0]
    scores = jnp.concatenate(
        [
            lax.dot_general(
                key_ref[source, 0, 0],
                query_t,
                (((0,), (0,)), ((), ())),
                preferred_element_type=jnp.float32,
            )
            for source in range(sources)
        ],
        axis=0,
    ) * scaling
    valid = mask_ref[...] > 0.5
    scores = jnp.where(valid, scores, -1e30)
    top = jnp.max(scores, axis=0, keepdims=True)
    weights_exp = jnp.exp(scores - top)
    total = jnp.sum(weights_exp, axis=0, keepdims=True)
    weights_low = weights_exp.astype(jnp.bfloat16)
    numer = jnp.zeros((HEAD_DIM, rows), jnp.float32)
    for source in range(sources):
        numer = numer + jnp.dot(
            value_ref[source, 0, 0],
            weights_low[source * rows : (source + 1) * rows],
            preferred_element_type=jnp.float32,
        )
    out_ref[0, 0] = (numer / total).astype(out_ref.dtype)


def attend(qkv, key_valid):
    sources, slots, rows = qkv.shape[0], qkv.shape[2], qkv.shape[4]
    mask = key_valid.astype(jnp.float32)[:, None]
    return pl.pallas_call(
        attention_kernel,
        grid=(slots, sources),
        in_specs=[
            pl.BlockSpec((sources * rows, 1), lambda h, i: (0, 0)),
            pl.BlockSpec((1, 1, 1, HEAD_DIM, rows), lambda h, i: (i, 0, h, 0, 0)),
            pl.BlockSpec((sources, 1, 1, HEAD_DIM, rows), lambda h, i: (0, 1, h, 0, 0)),
            pl.BlockSpec((sources, 1, 1, HEAD_DIM, rows), lambda h, i: (0, 2, h, 0, 0)),
        ],
        out_specs=pl.BlockSpec((1, 1, HEAD_DIM, rows), lambda h, i: (i, h, 0, 0)),
        out_shape=jax.ShapeDtypeStruct((sources, slots, HEAD_DIM, rows), jnp.bfloat16),
    )(mask, qkv, qkv, qkv)


def conv_kernel(taps_ref, rows_ref, out_ref, scratch_ref, *, start, count):
    scratch_ref[...] = rows_ref[0].astype(jnp.float32)
    total = jnp.zeros((count, out_ref.shape[2]), jnp.float32)
    for tap in range(KERNEL):
        total = total + taps_ref[tap : tap + 1, :].astype(jnp.float32) * scratch_ref[
            start + tap : start + tap + count, :
        ]
    out_ref[0] = total


def depthwise_conv(depthwise_taps, rows, start, count, lanes=256):
    blocks, height, width = rows.shape
    return pl.pallas_call(
        functools.partial(conv_kernel, start=start, count=count),
        grid=(blocks, width // lanes),
        in_specs=[
            pl.BlockSpec((KERNEL, lanes), lambda b, c: (0, c)),
            pl.BlockSpec((1, height, lanes), lambda b, c: (b, 0, c)),
        ],
        out_specs=pl.BlockSpec((1, count, lanes), lambda b, c: (b, 0, c)),
        out_shape=jax.ShapeDtypeStruct((blocks, count, width), jnp.float32),
        scratch_shapes=[pltpu.VMEM((height, lanes), jnp.float32)],
    )(depthwise_taps, rows)


def add_rows(left, piece):
    return jnp.dot(left, piece, preferred_element_type=jnp.float32)


def body(
    frames,
    routes,
    lengths,
    attention_gain,
    query_weight,
    key_weight,
    value_weight,
    output_weight,
    convolution_gain,
    pointwise_in,
    depthwise_taps,
    depthwise_gain,
    pointwise_out,
):
    shard_index = lax.axis_index("seq")
    blocks_here = frames.shape[1]
    block_rows = frames.shape[2]
    width = frames.shape[3]
    frame_rows = blocks_here * block_rows
    route_row = routes[0]
    own_places = lax.dynamic_slice_in_dim(route_row, shard_index * blocks_here, blocks_here)
    length = lengths[0]
    ordered = frames[0].reshape(frame_rows, width)
    positions = (own_places[:, None] * block_rows + jnp.arange(block_rows)[None, :]).reshape(
        frame_rows
    )
    is_valid = positions < length
    normed = layer_norm(ordered, attention_gain).astype(jnp.bfloat16)
    att_width = query_weight.shape[1]
    head_count = att_width // HEAD_DIM
    shards = lax.axis_size("seq")
    slots = -(-head_count // shards)
    qkv_local = jnp.concatenate([query_weight, key_weight, value_weight], axis=1)
    qkv_weight = lax.all_gather(qkv_local, "dp", axis=0, tiled=True)
    projected_t = lax.dot_general(
        qkv_weight, normed, (((0,), (1,)), ((), ())), preferred_element_type=jnp.float32
    ).astype(jnp.bfloat16)
    projected_t = projected_t.reshape(3, head_count, HEAD_DIM, frame_rows)
    projected_t = jnp.pad(
        projected_t, ((0, 0), (0, slots * shards - head_count), (0, 0), (0, 0))
    ).reshape(3, slots, shards, HEAD_DIM, frame_rows)
    outbound = projected_t.transpose(2, 0, 1, 3, 4)
    arrived = lax.all_to_all(outbound, "seq", split_axis=0, concat_axis=0, tiled=True)
    all_rows = shards * frame_rows
    key_positions = (
        route_row[:, None] * block_rows + jnp.arange(block_rows)[None, :]
    ).reshape(all_rows)
    key_valid = key_positions < length
    mixed = attend(arrived, key_valid)
    returned = lax.all_to_all(mixed, "seq", split_axis=0, concat_axis=0, tiled=True)
    attended = returned.transpose(3, 1, 0, 2).reshape(frame_rows, slots * shards * HEAD_DIM)
    attended = attended[:, :att_width]
    out_rows = output_weight.shape[0]
    in_width = pointwise_in.shape[1]
    late_local = jnp.concatenate(
        [
            output_weight.reshape(pointwise_in.shape[0], -1),
            pointwise_in,
            pointwise_out,
        ],
        axis=1,
    )
    late_weight = lax.all_gather(late_local, "dp", axis=0, tiled=True)
    out_cols = late_local.shape[1] - in_width - pointwise_out.shape[1]
    output_full = late_weight[:, :out_cols].reshape(-1, width)
    in_full = late_weight[:, out_cols : out_cols + in_width]
    out_full = late_weight[:, out_cols + in_width :]
    del out_rows
    half = KERNEL // 2
    middle = block_rows - 2 * EDGE

    def blocks_of(rows):
        return rows.reshape(blocks_here, block_rows, *rows.shape[1:])

    def edge_rows(rows):
        shaped = blocks_of(rows)
        return jnp.concatenate([shaped[:, :EDGE], shaped[:, block_rows - EDGE :]], axis=1)

    def middle_rows(rows):
        return blocks_of(rows)[:, EDGE : block_rows - EDGE]

    def frame_path(attended_rows, ordered_rows, valid_rows):
        count = attended_rows.shape[0] * attended_rows.shape[1]
        projected = add_rows(attended_rows.reshape(count, -1), output_full)
        after = (ordered_rows.reshape(count, width).astype(jnp.float32) + projected).astype(
            jnp.bfloat16
        )
        conv_normed = layer_norm(after, convolution_gain).astype(jnp.bfloat16)
        expanded = add_rows(conv_normed, in_full)
        gated = expanded[:, :width] * jax.nn.sigmoid(expanded[:, width:])
        gated = jnp.where(valid_rows.reshape(count)[:, None], gated, 0.0).astype(jnp.bfloat16)
        shape = attended_rows.shape[:2] + (width,)
        return after.reshape(shape), gated.reshape(shape)

    after_edge, edges = frame_path(edge_rows(attended), edge_rows(ordered), edge_rows(is_valid))
    all_edges = lax.all_gather(edges, "seq", axis=0, tiled=True)
    after_middle, gated_middle = frame_path(
        middle_rows(attended), middle_rows(ordered), middle_rows(is_valid)
    )
    gated_blocks = jnp.concatenate([edges[:, :EDGE], gated_middle, edges[:, EDGE:]], axis=1)
    after_blocks = jnp.concatenate(
        [after_edge[:, :EDGE], after_middle, after_edge[:, EDGE:]], axis=1
    )

    def convolve(padded, count):
        total = jnp.zeros((blocks_here, count, width), jnp.float32)
        for tap in range(KERNEL):
            total = total + depthwise_taps[tap].astype(jnp.float32)[None, None, :] * padded[
                :, tap : tap + count
            ].astype(jnp.float32)
        return total

    def finish(depthwise, after):
        count = depthwise.shape[0] * depthwise.shape[1]
        shaped = layer_norm(depthwise.reshape(count, width), depthwise_gain)
        activated = (shaped * jax.nn.sigmoid(shaped)).astype(jnp.bfloat16)
        contracted = add_rows(activated, out_full)
        result = (after.reshape(count, width).astype(jnp.float32) + contracted).astype(
            jnp.bfloat16
        )
        return result.reshape(depthwise.shape)

    inner = finish(
        depthwise_conv(depthwise_taps, gated_blocks, EDGE - half, middle),
        after_blocks[:, EDGE : block_rows - EDGE],
    )
    before = route_row[None, :] == (own_places[:, None] - 1)
    after = route_row[None, :] == (own_places[:, None] + 1)
    low = select_blocks(before, all_edges[:, EDGE:])[:, EDGE - half :]
    high = select_blocks(after, all_edges[:, :EDGE])[:, :half]
    low_conv = depthwise_conv(
        depthwise_taps,
        jnp.concatenate([low, gated_blocks[:, : 2 * EDGE + 1]], axis=1),
        0,
        EDGE,
    )
    high_conv = depthwise_conv(
        depthwise_taps,
        jnp.concatenate([gated_blocks[:, block_rows - 2 * EDGE - 1 :], high], axis=1),
        2,
        EDGE,
    )
    outer = finish(
        jnp.concatenate([low_conv, high_conv], axis=1),
        jnp.concatenate([after_blocks[:, :EDGE], after_blocks[:, block_rows - EDGE :]], axis=1),
    )
    result = jnp.concatenate([outer[:, :EDGE], inner, outer[:, EDGE:]], axis=1)
    del middle
    return result[None]


def solution(mesh):
    placed = (
        P("dp", "seq", None, None),
        P("dp", None),
        P("dp"),
        P(),
        P("dp", None),
        P("dp", None),
        P("dp", None),
        P("dp", None),
        P(),
        P("dp", None),
        P(),
        P(),
        P("dp", None),
    )
    return jax.shard_map(
        body, mesh=mesh, in_specs=placed, out_specs=P("dp", "seq", None, None), check_vma=False
    )
```

```python
import math

import jax
import jax.numpy as jnp
from jax import lax
from jax.experimental import pallas as pl
from jax.sharding import PartitionSpec as P

HEAD_DIM = 64
KERNEL = 31
EDGE = 16


def layer_norm(values, gain_row):
    values = values.astype(jnp.float32)
    center = values - jnp.mean(values, axis=-1, keepdims=True)
    spread = jnp.mean(center * center, axis=-1, keepdims=True)
    return center * lax.rsqrt(spread + 1e-05) * gain_row


def select_blocks(selector, blocks):
    return jnp.einsum(
        "ab,bfc->afc", selector.astype(jnp.bfloat16), blocks, preferred_element_type=jnp.float32
    ).astype(jnp.bfloat16)


def attention_kernel(mask_ref, query_ref, key_ref, value_ref, out_ref):
    scaling = 1.0 / math.sqrt(HEAD_DIM)
    sources, rows = key_ref.shape[0], key_ref.shape[4]
    valid = mask_ref[...] > 0.5
    for part in range(query_ref.shape[0]):
        query_t = query_ref[part, 0, 0]
        scores = jnp.concatenate(
            [
                lax.dot_general(
                    key_ref[source, 0, 0],
                    query_t,
                    (((0,), (0,)), ((), ())),
                    preferred_element_type=jnp.float32,
                )
                for source in range(sources)
            ],
            axis=0,
        ) * scaling
        scores = jnp.where(valid, scores, -1e30)
        top = jnp.max(scores, axis=0, keepdims=True)
        weights_exp = jnp.exp(scores - top)
        total = jnp.sum(weights_exp, axis=0, keepdims=True)
        weights_low = weights_exp.astype(jnp.bfloat16)
        numer = jnp.zeros((HEAD_DIM, rows), jnp.float32)
        for source in range(sources):
            numer = numer + jnp.dot(
                value_ref[source, 0, 0],
                weights_low[source * rows : (source + 1) * rows],
                preferred_element_type=jnp.float32,
            )
        out_ref[part, 0] = (numer / total).astype(out_ref.dtype)


def attend(qkv, key_valid, per_step=2):
    sources, slots, rows = qkv.shape[0], qkv.shape[2], qkv.shape[4]
    mask = key_valid.astype(jnp.float32)[:, None]
    return pl.pallas_call(
        attention_kernel,
        grid=(slots, sources // per_step),
        in_specs=[
            pl.BlockSpec((sources * rows, 1), lambda h, i: (0, 0)),
            pl.BlockSpec((per_step, 1, 1, HEAD_DIM, rows), lambda h, i: (i, 0, h, 0, 0)),
            pl.BlockSpec((sources, 1, 1, HEAD_DIM, rows), lambda h, i: (0, 1, h, 0, 0)),
            pl.BlockSpec((sources, 1, 1, HEAD_DIM, rows), lambda h, i: (0, 2, h, 0, 0)),
        ],
        out_specs=pl.BlockSpec((per_step, 1, HEAD_DIM, rows), lambda h, i: (i, h, 0, 0)),
        out_shape=jax.ShapeDtypeStruct((sources, slots, HEAD_DIM, rows), jnp.bfloat16),
    )(mask, qkv, qkv, qkv)


def add_rows(left, piece):
    return jnp.dot(left, piece, preferred_element_type=jnp.float32)


def body(
    frames,
    routes,
    lengths,
    attention_gain,
    query_weight,
    key_weight,
    value_weight,
    output_weight,
    convolution_gain,
    pointwise_in,
    depthwise_taps,
    depthwise_gain,
    pointwise_out,
):
    shard_index = lax.axis_index("seq")
    blocks_here = frames.shape[1]
    block_rows = frames.shape[2]
    width = frames.shape[3]
    frame_rows = blocks_here * block_rows
    route_row = routes[0]
    own_places = lax.dynamic_slice_in_dim(route_row, shard_index * blocks_here, blocks_here)
    length = lengths[0]
    ordered = frames[0].reshape(frame_rows, width)
    positions = (own_places[:, None] * block_rows + jnp.arange(block_rows)[None, :]).reshape(
        frame_rows
    )
    is_valid = positions < length
    normed = layer_norm(ordered, attention_gain).astype(jnp.bfloat16)
    att_width = query_weight.shape[1]
    head_count = att_width // HEAD_DIM
    shards = lax.axis_size("seq")
    slots = -(-head_count // shards)
    qkv_local = jnp.concatenate([query_weight, key_weight, value_weight], axis=1)
    qkv_weight = lax.all_gather(qkv_local, "dp", axis=0, tiled=True)
    projected_t = lax.dot_general(
        qkv_weight, normed, (((0,), (1,)), ((), ())), preferred_element_type=jnp.float32
    ).astype(jnp.bfloat16)
    projected_t = projected_t.reshape(3, head_count, HEAD_DIM, frame_rows)
    projected_t = jnp.pad(
        projected_t, ((0, 0), (0, slots * shards - head_count), (0, 0), (0, 0))
    ).reshape(3, slots, shards, HEAD_DIM, frame_rows)
    outbound = projected_t.transpose(2, 0, 1, 3, 4)
    arrived = lax.all_to_all(outbound, "seq", split_axis=0, concat_axis=0, tiled=True)
    all_rows = shards * frame_rows
    key_positions = (
        route_row[:, None] * block_rows + jnp.arange(block_rows)[None, :]
    ).reshape(all_rows)
    key_valid = key_positions < length
    mixed = attend(arrived, key_valid)
    returned = lax.all_to_all(mixed, "seq", split_axis=0, concat_axis=0, tiled=True)
    attended = returned.transpose(3, 1, 0, 2).reshape(frame_rows, slots * shards * HEAD_DIM)
    attended = attended[:, :att_width]
    out_rows = output_weight.shape[0]
    in_width = pointwise_in.shape[1]
    late_local = jnp.concatenate(
        [
            output_weight.reshape(pointwise_in.shape[0], -1),
            pointwise_in,
            pointwise_out,
        ],
        axis=1,
    )
    late_weight = lax.all_gather(late_local, "dp", axis=0, tiled=True)
    out_cols = late_local.shape[1] - in_width - pointwise_out.shape[1]
    output_full = late_weight[:, :out_cols].reshape(-1, width)
    in_full = late_weight[:, out_cols : out_cols + in_width]
    out_full = late_weight[:, out_cols + in_width :]
    del out_rows
    half = KERNEL // 2
    middle = block_rows - 2 * EDGE

    def blocks_of(rows):
        return rows.reshape(blocks_here, block_rows, *rows.shape[1:])

    def edge_rows(rows):
        shaped = blocks_of(rows)
        return jnp.concatenate([shaped[:, :EDGE], shaped[:, block_rows - EDGE :]], axis=1)

    def middle_rows(rows):
        return blocks_of(rows)[:, EDGE : block_rows - EDGE]

    def frame_path(attended_rows, ordered_rows, valid_rows):
        count = attended_rows.shape[0] * attended_rows.shape[1]
        projected = add_rows(attended_rows.reshape(count, -1), output_full)
        after = (ordered_rows.reshape(count, width).astype(jnp.float32) + projected).astype(
            jnp.bfloat16
        )
        conv_normed = layer_norm(after, convolution_gain).astype(jnp.bfloat16)
        expanded = add_rows(conv_normed, in_full)
        gated = expanded[:, :width] * jax.nn.sigmoid(expanded[:, width:])
        gated = jnp.where(valid_rows.reshape(count)[:, None], gated, 0.0).astype(jnp.bfloat16)
        shape = attended_rows.shape[:2] + (width,)
        return after.reshape(shape), gated.reshape(shape)

    after_edge, edges = frame_path(edge_rows(attended), edge_rows(ordered), edge_rows(is_valid))
    all_edges = lax.all_gather(edges, "seq", axis=0, tiled=True)
    after_middle, gated_middle = frame_path(
        middle_rows(attended), middle_rows(ordered), middle_rows(is_valid)
    )
    gated_blocks = jnp.concatenate([edges[:, :EDGE], gated_middle, edges[:, EDGE:]], axis=1)
    after_blocks = jnp.concatenate(
        [after_edge[:, :EDGE], after_middle, after_edge[:, EDGE:]], axis=1
    )

    def convolve(padded, count):
        total = jnp.zeros((blocks_here, count, width), jnp.float32)
        for tap in range(KERNEL):
            total = total + depthwise_taps[tap].astype(jnp.float32)[None, None, :] * padded[
                :, tap : tap + count
            ].astype(jnp.float32)
        return total

    def finish(depthwise, after):
        count = depthwise.shape[0] * depthwise.shape[1]
        shaped = layer_norm(depthwise.reshape(count, width), depthwise_gain)
        activated = (shaped * jax.nn.sigmoid(shaped)).astype(jnp.bfloat16)
        contracted = add_rows(activated, out_full)
        result = (after.reshape(count, width).astype(jnp.float32) + contracted).astype(
            jnp.bfloat16
        )
        return result.reshape(depthwise.shape)

    inner = finish(
        convolve(gated_blocks[:, EDGE - half :], middle), after_blocks[:, EDGE : block_rows - EDGE]
    )
    before = route_row[None, :] == (own_places[:, None] - 1)
    after = route_row[None, :] == (own_places[:, None] + 1)
    low = select_blocks(before, all_edges[:, EDGE:])[:, EDGE - half :]
    high = select_blocks(after, all_edges[:, :EDGE])[:, :half]
    low_conv = convolve(jnp.concatenate([low, gated_blocks[:, : EDGE + half]], axis=1), EDGE)
    high_conv = convolve(
        jnp.concatenate([gated_blocks[:, block_rows - EDGE - half :], high], axis=1), EDGE
    )
    outer = finish(
        jnp.concatenate([low_conv, high_conv], axis=1),
        jnp.concatenate([after_blocks[:, :EDGE], after_blocks[:, block_rows - EDGE :]], axis=1),
    )
    result = jnp.concatenate([outer[:, :EDGE], inner, outer[:, EDGE:]], axis=1)
    del middle
    return result[None]


def solution(mesh):
    placed = (
        P("dp", "seq", None, None),
        P("dp", None),
        P("dp"),
        P(),
        P("dp", None),
        P("dp", None),
        P("dp", None),
        P("dp", None),
        P(),
        P("dp", None),
        P(),
        P(),
        P("dp", None),
    )
    return jax.shard_map(
        body, mesh=mesh, in_specs=placed, out_specs=P("dp", "seq", None, None), check_vma=False
    )
```

```python
import math

import jax
import jax.numpy as jnp
from jax import lax
from jax.experimental import pallas as pl
from jax.sharding import PartitionSpec as P

HEAD_DIM = 64
KERNEL = 31
EDGE = 16


def layer_norm(values, gain_row):
    values = values.astype(jnp.float32)
    center = values - jnp.mean(values, axis=-1, keepdims=True)
    spread = jnp.mean(center * center, axis=-1, keepdims=True)
    return center * lax.rsqrt(spread + 1e-05) * gain_row


def select_blocks(selector, blocks):
    return jnp.einsum(
        "ab,bfc->afc", selector.astype(jnp.bfloat16), blocks, preferred_element_type=jnp.float32
    ).astype(jnp.bfloat16)


def attention_kernel(mask_ref, query_ref, key_ref, value_ref, out_ref):
    scaling = 1.0 / math.sqrt(HEAD_DIM)
    sources, rows = key_ref.shape[0], key_ref.shape[4]
    valid = mask_ref[...] > 0.5
    for part in range(query_ref.shape[0]):
        query_t = query_ref[part, 0, 0]
        scores = jnp.concatenate(
            [
                lax.dot_general(
                    key_ref[source, 0, 0],
                    query_t,
                    (((0,), (0,)), ((), ())),
                    preferred_element_type=jnp.float32,
                )
                for source in range(sources)
            ],
            axis=0,
        ) * scaling
        scores = jnp.where(valid, scores, -1e30)
        top = jnp.max(scores, axis=0, keepdims=True)
        weights_exp = jnp.exp(scores - top)
        total = jnp.sum(weights_exp, axis=0, keepdims=True)
        weights_low = weights_exp.astype(jnp.bfloat16)
        numer = jnp.zeros((HEAD_DIM, rows), jnp.float32)
        for source in range(sources):
            numer = numer + jnp.dot(
                value_ref[source, 0, 0],
                weights_low[source * rows : (source + 1) * rows],
                preferred_element_type=jnp.float32,
            )
        out_ref[part, 0] = (numer / total).astype(out_ref.dtype)


def attend(qkv, key_valid, per_step=2):
    sources, slots, rows = qkv.shape[0], qkv.shape[2], qkv.shape[4]
    mask = key_valid.astype(jnp.float32)[:, None]
    return pl.pallas_call(
        attention_kernel,
        grid=(slots, sources // per_step),
        in_specs=[
            pl.BlockSpec((sources * rows, 1), lambda h, i: (0, 0)),
            pl.BlockSpec((per_step, 1, 1, HEAD_DIM, rows), lambda h, i: (i, 0, h, 0, 0)),
            pl.BlockSpec((sources, 1, 1, HEAD_DIM, rows), lambda h, i: (0, 1, h, 0, 0)),
            pl.BlockSpec((sources, 1, 1, HEAD_DIM, rows), lambda h, i: (0, 2, h, 0, 0)),
        ],
        out_specs=pl.BlockSpec((per_step, 1, HEAD_DIM, rows), lambda h, i: (i, h, 0, 0)),
        out_shape=jax.ShapeDtypeStruct((sources, slots, HEAD_DIM, rows), jnp.bfloat16),
    )(mask, qkv, qkv, qkv)


def add_rows(left, piece):
    return jnp.dot(left, piece, preferred_element_type=jnp.float32)


def body(
    frames,
    routes,
    lengths,
    attention_gain,
    query_weight,
    key_weight,
    value_weight,
    output_weight,
    convolution_gain,
    pointwise_in,
    depthwise_taps,
    depthwise_gain,
    pointwise_out,
):
    shard_index = lax.axis_index("seq")
    blocks_here = frames.shape[1]
    block_rows = frames.shape[2]
    width = frames.shape[3]
    frame_rows = blocks_here * block_rows
    route_row = routes[0]
    own_places = lax.dynamic_slice_in_dim(route_row, shard_index * blocks_here, blocks_here)
    length = lengths[0]
    ordered = frames[0].reshape(frame_rows, width)
    positions = (own_places[:, None] * block_rows + jnp.arange(block_rows)[None, :]).reshape(
        frame_rows
    )
    is_valid = positions < length
    normed = layer_norm(ordered, attention_gain).astype(jnp.bfloat16)
    att_width = query_weight.shape[1]
    head_count = att_width // HEAD_DIM
    shards = lax.axis_size("seq")
    slots = -(-head_count // shards)
    qkv_local = jnp.zeros(
        (query_weight.shape[0], 3 * att_width), query_weight.dtype
    )
    for index, kind in enumerate((query_weight, key_weight, value_weight)):
        qkv_local = lax.dynamic_update_slice(qkv_local, kind, (0, index * att_width))
    qkv_weight = lax.all_gather(qkv_local, "dp", axis=0, tiled=True)
    projected_t = lax.dot_general(
        qkv_weight, normed, (((0,), (1,)), ((), ())), preferred_element_type=jnp.float32
    ).astype(jnp.bfloat16)
    projected_t = projected_t.reshape(3, head_count, HEAD_DIM, frame_rows)
    projected_t = jnp.pad(
        projected_t, ((0, 0), (0, slots * shards - head_count), (0, 0), (0, 0))
    ).reshape(3, slots, shards, HEAD_DIM, frame_rows)
    outbound = projected_t.transpose(2, 0, 1, 3, 4)
    arrived = lax.all_to_all(outbound, "seq", split_axis=0, concat_axis=0, tiled=True)
    all_rows = shards * frame_rows
    key_positions = (
        route_row[:, None] * block_rows + jnp.arange(block_rows)[None, :]
    ).reshape(all_rows)
    key_valid = key_positions < length
    mixed = attend(arrived, key_valid)
    returned = lax.all_to_all(mixed, "seq", split_axis=0, concat_axis=0, tiled=True)
    attended = returned.transpose(3, 1, 0, 2).reshape(frame_rows, slots * shards * HEAD_DIM)
    attended = attended[:, :att_width]
    out_rows = output_weight.shape[0]
    in_width = pointwise_in.shape[1]
    late_local = jnp.concatenate(
        [
            output_weight.reshape(pointwise_in.shape[0], -1),
            pointwise_in,
            pointwise_out,
        ],
        axis=1,
    )
    late_weight = lax.all_gather(late_local, "dp", axis=0, tiled=True)
    out_cols = late_local.shape[1] - in_width - pointwise_out.shape[1]
    output_full = late_weight[:, :out_cols].reshape(-1, width)
    in_full = late_weight[:, out_cols : out_cols + in_width]
    out_full = late_weight[:, out_cols + in_width :]
    del out_rows
    half = KERNEL // 2
    middle = block_rows - 2 * EDGE

    def blocks_of(rows):
        return rows.reshape(blocks_here, block_rows, *rows.shape[1:])

    def edge_rows(rows):
        shaped = blocks_of(rows)
        return jnp.concatenate([shaped[:, :EDGE], shaped[:, block_rows - EDGE :]], axis=1)

    def middle_rows(rows):
        return blocks_of(rows)[:, EDGE : block_rows - EDGE]

    def frame_path(attended_rows, ordered_rows, valid_rows):
        count = attended_rows.shape[0] * attended_rows.shape[1]
        projected = add_rows(attended_rows.reshape(count, -1), output_full)
        after = (ordered_rows.reshape(count, width).astype(jnp.float32) + projected).astype(
            jnp.bfloat16
        )
        conv_normed = layer_norm(after, convolution_gain).astype(jnp.bfloat16)
        expanded = add_rows(conv_normed, in_full)
        gated = expanded[:, :width] * jax.nn.sigmoid(expanded[:, width:])
        gated = jnp.where(valid_rows.reshape(count)[:, None], gated, 0.0).astype(jnp.bfloat16)
        shape = attended_rows.shape[:2] + (width,)
        return after.reshape(shape), gated.reshape(shape)

    after_edge, edges = frame_path(edge_rows(attended), edge_rows(ordered), edge_rows(is_valid))
    all_edges = lax.all_gather(edges, "seq", axis=0, tiled=True)
    after_middle, gated_middle = frame_path(
        middle_rows(attended), middle_rows(ordered), middle_rows(is_valid)
    )
    gated_blocks = jnp.concatenate([edges[:, :EDGE], gated_middle, edges[:, EDGE:]], axis=1)
    after_blocks = jnp.concatenate(
        [after_edge[:, :EDGE], after_middle, after_edge[:, EDGE:]], axis=1
    )

    def convolve(padded, count):
        total = jnp.zeros((blocks_here, count, width), jnp.float32)
        for tap in range(KERNEL):
            total = total + depthwise_taps[tap].astype(jnp.float32)[None, None, :] * padded[
                :, tap : tap + count
            ].astype(jnp.float32)
        return total

    def finish(depthwise, after):
        count = depthwise.shape[0] * depthwise.shape[1]
        shaped = layer_norm(depthwise.reshape(count, width), depthwise_gain)
        activated = (shaped * jax.nn.sigmoid(shaped)).astype(jnp.bfloat16)
        contracted = add_rows(activated, out_full)
        result = (after.reshape(count, width).astype(jnp.float32) + contracted).astype(
            jnp.bfloat16
        )
        return result.reshape(depthwise.shape)

    inner = finish(
        convolve(gated_blocks[:, EDGE - half :], middle), after_blocks[:, EDGE : block_rows - EDGE]
    )
    before = route_row[None, :] == (own_places[:, None] - 1)
    after = route_row[None, :] == (own_places[:, None] + 1)
    low = select_blocks(before, all_edges[:, EDGE:])[:, EDGE - half :]
    high = select_blocks(after, all_edges[:, :EDGE])[:, :half]
    low_conv = convolve(jnp.concatenate([low, gated_blocks[:, : EDGE + half]], axis=1), EDGE)
    high_conv = convolve(
        jnp.concatenate([gated_blocks[:, block_rows - EDGE - half :], high], axis=1), EDGE
    )
    outer = finish(
        jnp.concatenate([low_conv, high_conv], axis=1),
        jnp.concatenate([after_blocks[:, :EDGE], after_blocks[:, block_rows - EDGE :]], axis=1),
    )
    result = jnp.concatenate([outer[:, :EDGE], inner, outer[:, EDGE:]], axis=1)
    del middle
    return result[None]


def solution(mesh):
    placed = (
        P("dp", "seq", None, None),
        P("dp", None),
        P("dp"),
        P(),
        P("dp", None),
        P("dp", None),
        P("dp", None),
        P("dp", None),
        P(),
        P("dp", None),
        P(),
        P(),
        P("dp", None),
    )
    return jax.shard_map(
        body, mesh=mesh, in_specs=placed, out_specs=P("dp", "seq", None, None), check_vma=False
    )
```

```python
import math

import jax
import jax.numpy as jnp
from jax import lax
from jax.experimental import pallas as pl
from jax.sharding import PartitionSpec as P

HEAD_DIM = 64
KERNEL = 31
EDGE = 16


def layer_norm(values, gain_row):
    values = values.astype(jnp.float32)
    center = values - jnp.mean(values, axis=-1, keepdims=True)
    spread = jnp.mean(center * center, axis=-1, keepdims=True)
    return center * lax.rsqrt(spread + 1e-05) * gain_row


def select_blocks(selector, blocks):
    return jnp.einsum(
        "ab,bfc->afc", selector.astype(jnp.bfloat16), blocks, preferred_element_type=jnp.float32
    ).astype(jnp.bfloat16)


def attention_kernel(mask_ref, query_ref, key_ref, value_ref, out_ref):
    scaling = 1.0 / math.sqrt(HEAD_DIM)
    sources, rows = key_ref.shape[0], key_ref.shape[4]
    valid = mask_ref[...] > 0.5
    for part in range(query_ref.shape[0]):
        query_t = query_ref[part, 0, 0]
        scores = jnp.concatenate(
            [
                lax.dot_general(
                    key_ref[source, 0, 0],
                    query_t,
                    (((0,), (0,)), ((), ())),
                    preferred_element_type=jnp.float32,
                )
                for source in range(sources)
            ],
            axis=0,
        ) * scaling
        scores = jnp.where(valid, scores, -1e30)
        top = jnp.max(scores, axis=0, keepdims=True)
        weights_exp = jnp.exp(scores - top)
        total = jnp.sum(weights_exp, axis=0, keepdims=True)
        weights_low = weights_exp.astype(jnp.bfloat16)
        numer = jnp.zeros((HEAD_DIM, rows), jnp.float32)
        for source in range(sources):
            numer = numer + jnp.dot(
                value_ref[source, 0, 0],
                weights_low[source * rows : (source + 1) * rows],
                preferred_element_type=jnp.float32,
            )
        out_ref[part, 0] = (numer / total).astype(out_ref.dtype)


def attend(qkv, key_valid, per_step=4):
    sources, slots, rows = qkv.shape[0], qkv.shape[2], qkv.shape[4]
    mask = key_valid.astype(jnp.float32)[:, None]
    return pl.pallas_call(
        attention_kernel,
        grid=(slots, sources // per_step),
        in_specs=[
            pl.BlockSpec((sources * rows, 1), lambda h, i: (0, 0)),
            pl.BlockSpec((per_step, 1, 1, HEAD_DIM, rows), lambda h, i: (i, 0, h, 0, 0)),
            pl.BlockSpec((sources, 1, 1, HEAD_DIM, rows), lambda h, i: (0, 1, h, 0, 0)),
            pl.BlockSpec((sources, 1, 1, HEAD_DIM, rows), lambda h, i: (0, 2, h, 0, 0)),
        ],
        out_specs=pl.BlockSpec((per_step, 1, HEAD_DIM, rows), lambda h, i: (i, h, 0, 0)),
        out_shape=jax.ShapeDtypeStruct((sources, slots, HEAD_DIM, rows), jnp.bfloat16),
    )(mask, qkv, qkv, qkv)


def add_rows(left, piece):
    return jnp.dot(left, piece, preferred_element_type=jnp.float32)


def body(
    frames,
    routes,
    lengths,
    attention_gain,
    query_weight,
    key_weight,
    value_weight,
    output_weight,
    convolution_gain,
    pointwise_in,
    depthwise_taps,
    depthwise_gain,
    pointwise_out,
):
    shard_index = lax.axis_index("seq")
    blocks_here = frames.shape[1]
    block_rows = frames.shape[2]
    width = frames.shape[3]
    frame_rows = blocks_here * block_rows
    route_row = routes[0]
    own_places = lax.dynamic_slice_in_dim(route_row, shard_index * blocks_here, blocks_here)
    length = lengths[0]
    ordered = frames[0].reshape(frame_rows, width)
    positions = (own_places[:, None] * block_rows + jnp.arange(block_rows)[None, :]).reshape(
        frame_rows
    )
    is_valid = positions < length
    normed = layer_norm(ordered, attention_gain).astype(jnp.bfloat16)
    att_width = query_weight.shape[1]
    head_count = att_width // HEAD_DIM
    shards = lax.axis_size("seq")
    slots = -(-head_count // shards)
    qkv_local = jnp.concatenate([query_weight, key_weight, value_weight], axis=1)
    qkv_weight = lax.all_gather(qkv_local, "dp", axis=0, tiled=True)
    projected_t = lax.dot_general(
        qkv_weight, normed, (((0,), (1,)), ((), ())), preferred_element_type=jnp.float32
    ).astype(jnp.bfloat16)
    projected_t = projected_t.reshape(3, head_count, HEAD_DIM, frame_rows)
    projected_t = jnp.pad(
        projected_t, ((0, 0), (0, slots * shards - head_count), (0, 0), (0, 0))
    ).reshape(3, slots, shards, HEAD_DIM, frame_rows)
    outbound = projected_t.transpose(2, 0, 1, 3, 4)
    arrived = lax.all_to_all(outbound, "seq", split_axis=0, concat_axis=0, tiled=True)
    all_rows = shards * frame_rows
    key_positions = (
        route_row[:, None] * block_rows + jnp.arange(block_rows)[None, :]
    ).reshape(all_rows)
    key_valid = key_positions < length
    mixed = attend(arrived, key_valid)
    returned = lax.all_to_all(mixed, "seq", split_axis=0, concat_axis=0, tiled=True)
    attended = returned.transpose(3, 1, 0, 2).reshape(frame_rows, slots * shards * HEAD_DIM)
    attended = attended[:, :att_width]
    out_rows = output_weight.shape[0]
    in_width = pointwise_in.shape[1]
    late_local = jnp.concatenate(
        [
            output_weight.reshape(pointwise_in.shape[0], -1),
            pointwise_in,
            pointwise_out,
        ],
        axis=1,
    )
    late_weight = lax.all_gather(late_local, "dp", axis=0, tiled=True)
    out_cols = late_local.shape[1] - in_width - pointwise_out.shape[1]
    output_full = late_weight[:, :out_cols].reshape(-1, width)
    in_full = late_weight[:, out_cols : out_cols + in_width]
    out_full = late_weight[:, out_cols + in_width :]
    del out_rows
    half = KERNEL // 2
    middle = block_rows - 2 * EDGE

    def blocks_of(rows):
        return rows.reshape(blocks_here, block_rows, *rows.shape[1:])

    def edge_rows(rows):
        shaped = blocks_of(rows)
        return jnp.concatenate([shaped[:, :EDGE], shaped[:, block_rows - EDGE :]], axis=1)

    def middle_rows(rows):
        return blocks_of(rows)[:, EDGE : block_rows - EDGE]

    def frame_path(attended_rows, ordered_rows, valid_rows):
        count = attended_rows.shape[0] * attended_rows.shape[1]
        projected = add_rows(attended_rows.reshape(count, -1), output_full)
        after = (ordered_rows.reshape(count, width).astype(jnp.float32) + projected).astype(
            jnp.bfloat16
        )
        conv_normed = layer_norm(after, convolution_gain).astype(jnp.bfloat16)
        expanded = add_rows(conv_normed, in_full)
        gated = expanded[:, :width] * jax.nn.sigmoid(expanded[:, width:])
        gated = jnp.where(valid_rows.reshape(count)[:, None], gated, 0.0).astype(jnp.bfloat16)
        shape = attended_rows.shape[:2] + (width,)
        return after.reshape(shape), gated.reshape(shape)

    after_edge, edges = frame_path(edge_rows(attended), edge_rows(ordered), edge_rows(is_valid))
    all_edges = lax.all_gather(edges, "seq", axis=0, tiled=True)
    after_middle, gated_middle = frame_path(
        middle_rows(attended), middle_rows(ordered), middle_rows(is_valid)
    )
    gated_blocks = jnp.concatenate([edges[:, :EDGE], gated_middle, edges[:, EDGE:]], axis=1)
    after_blocks = jnp.concatenate(
        [after_edge[:, :EDGE], after_middle, after_edge[:, EDGE:]], axis=1
    )

    def convolve(padded, count):
        total = jnp.zeros((blocks_here, count, width), jnp.float32)
        for tap in range(KERNEL):
            total = total + depthwise_taps[tap].astype(jnp.float32)[None, None, :] * padded[
                :, tap : tap + count
            ].astype(jnp.float32)
        return total

    def finish(depthwise, after):
        count = depthwise.shape[0] * depthwise.shape[1]
        shaped = layer_norm(depthwise.reshape(count, width), depthwise_gain)
        activated = (shaped * jax.nn.sigmoid(shaped)).astype(jnp.bfloat16)
        contracted = add_rows(activated, out_full)
        result = (after.reshape(count, width).astype(jnp.float32) + contracted).astype(
            jnp.bfloat16
        )
        return result.reshape(depthwise.shape)

    inner = finish(
        convolve(gated_blocks[:, EDGE - half :], middle), after_blocks[:, EDGE : block_rows - EDGE]
    )
    before = route_row[None, :] == (own_places[:, None] - 1)
    after = route_row[None, :] == (own_places[:, None] + 1)
    low = select_blocks(before, all_edges[:, EDGE:])[:, EDGE - half :]
    high = select_blocks(after, all_edges[:, :EDGE])[:, :half]
    low_conv = convolve(jnp.concatenate([low, gated_blocks[:, : EDGE + half]], axis=1), EDGE)
    high_conv = convolve(
        jnp.concatenate([gated_blocks[:, block_rows - EDGE - half :], high], axis=1), EDGE
    )
    outer = finish(
        jnp.concatenate([low_conv, high_conv], axis=1),
        jnp.concatenate([after_blocks[:, :EDGE], after_blocks[:, block_rows - EDGE :]], axis=1),
    )
    result = jnp.concatenate([outer[:, :EDGE], inner, outer[:, EDGE:]], axis=1)
    del middle
    return result[None]


def solution(mesh):
    placed = (
        P("dp", "seq", None, None),
        P("dp", None),
        P("dp"),
        P(),
        P("dp", None),
        P("dp", None),
        P("dp", None),
        P("dp", None),
        P(),
        P("dp", None),
        P(),
        P(),
        P("dp", None),
    )
    return jax.shard_map(
        body, mesh=mesh, in_specs=placed, out_specs=P("dp", "seq", None, None), check_vma=False
    )
```

```python
import math

import jax
import jax.numpy as jnp
from jax import lax
from jax.experimental import pallas as pl
from jax.sharding import PartitionSpec as P

HEAD_DIM = 64
KERNEL = 31
EDGE = 16


def layer_norm(values, gain_row):
    values = values.astype(jnp.float32)
    center = values - jnp.mean(values, axis=-1, keepdims=True)
    spread = jnp.mean(center * center, axis=-1, keepdims=True)
    return center * lax.rsqrt(spread + 1e-05) * gain_row


def select_blocks(selector, blocks):
    return jnp.einsum(
        "ab,bfc->afc", selector.astype(jnp.bfloat16), blocks, preferred_element_type=jnp.float32
    ).astype(jnp.bfloat16)


def attention_kernel(mask_ref, query_ref, key_ref, value_ref, out_ref):
    scaling = 1.0 / math.sqrt(HEAD_DIM)
    sources, rows = key_ref.shape[0], key_ref.shape[4]
    valid = mask_ref[...] > 0.5
    for part in range(query_ref.shape[0]):
        query_t = query_ref[part, 0, 0]
        scores = jnp.concatenate(
            [
                lax.dot_general(
                    key_ref[source, 0, 0],
                    query_t,
                    (((0,), (0,)), ((), ())),
                    preferred_element_type=jnp.float32,
                )
                for source in range(sources)
            ],
            axis=0,
        ) * scaling
        scores = jnp.where(valid, scores, -1e30)
        top = jnp.max(scores, axis=0, keepdims=True)
        weights_exp = jnp.exp(scores - top)
        total = jnp.sum(weights_exp, axis=0, keepdims=True)
        weights_low = weights_exp.astype(jnp.bfloat16)
        numer = jnp.zeros((HEAD_DIM, rows), jnp.float32)
        for source in range(sources):
            numer = numer + jnp.dot(
                value_ref[source, 0, 0],
                weights_low[source * rows : (source + 1) * rows],
                preferred_element_type=jnp.float32,
            )
        out_ref[part, 0] = (numer / total).astype(out_ref.dtype)


def attend(qkv, key_valid, per_step=4):
    sources, slots, rows = qkv.shape[0], qkv.shape[2], qkv.shape[4]
    mask = key_valid.astype(jnp.float32)[:, None]
    return pl.pallas_call(
        attention_kernel,
        grid=(slots, sources // per_step),
        in_specs=[
            pl.BlockSpec((sources * rows, 1), lambda h, i: (0, 0)),
            pl.BlockSpec((per_step, 1, 1, HEAD_DIM, rows), lambda h, i: (i, 0, h, 0, 0)),
            pl.BlockSpec((sources, 1, 1, HEAD_DIM, rows), lambda h, i: (0, 1, h, 0, 0)),
            pl.BlockSpec((sources, 1, 1, HEAD_DIM, rows), lambda h, i: (0, 2, h, 0, 0)),
        ],
        out_specs=pl.BlockSpec((per_step, 1, HEAD_DIM, rows), lambda h, i: (i, h, 0, 0)),
        out_shape=jax.ShapeDtypeStruct((sources, slots, HEAD_DIM, rows), jnp.bfloat16),
    )(mask, qkv, qkv, qkv)


def add_rows(left, piece):
    return jnp.dot(left, piece, preferred_element_type=jnp.float32)


def body(
    frames,
    routes,
    lengths,
    attention_gain,
    query_weight,
    key_weight,
    value_weight,
    output_weight,
    convolution_gain,
    pointwise_in,
    depthwise_taps,
    depthwise_gain,
    pointwise_out,
):
    shard_index = lax.axis_index("seq")
    blocks_here = frames.shape[1]
    block_rows = frames.shape[2]
    width = frames.shape[3]
    frame_rows = blocks_here * block_rows
    route_row = routes[0]
    own_places = lax.dynamic_slice_in_dim(route_row, shard_index * blocks_here, blocks_here)
    length = lengths[0]
    ordered = frames[0].reshape(frame_rows, width)
    positions = (own_places[:, None] * block_rows + jnp.arange(block_rows)[None, :]).reshape(
        frame_rows
    )
    is_valid = positions < length
    normed = layer_norm(ordered, attention_gain).astype(jnp.bfloat16)
    att_width = query_weight.shape[1]
    head_count = att_width // HEAD_DIM
    shards = lax.axis_size("seq")
    slots = -(-head_count // shards)
    qkv_local = jnp.concatenate([query_weight, key_weight, value_weight], axis=1)
    qkv_weight = lax.all_gather(qkv_local, "dp", axis=0, tiled=True)
    projected_t = lax.dot_general(
        qkv_weight, normed, (((0,), (1,)), ((), ())), preferred_element_type=jnp.float32
    ).astype(jnp.bfloat16)
    projected_t = projected_t.reshape(3, head_count, HEAD_DIM, frame_rows)
    projected_t = jnp.pad(
        projected_t, ((0, 0), (0, slots * shards - head_count), (0, 0), (0, 0))
    ).reshape(3, slots, shards, HEAD_DIM, frame_rows)
    outbound = projected_t.transpose(2, 0, 1, 3, 4)
    arrived = lax.all_to_all(outbound, "seq", split_axis=0, concat_axis=0, tiled=True)
    all_rows = shards * frame_rows
    key_positions = (
        route_row[:, None] * block_rows + jnp.arange(block_rows)[None, :]
    ).reshape(all_rows)
    key_valid = key_positions < length
    mixed = attend(arrived, key_valid)
    returned = lax.all_to_all(mixed, "seq", split_axis=0, concat_axis=0, tiled=True)
    attended = returned.transpose(3, 1, 0, 2).reshape(frame_rows, slots * shards * HEAD_DIM)
    attended = attended[:, :att_width]
    out_rows = output_weight.shape[0]
    in_width = pointwise_in.shape[1]
    late_local = jnp.concatenate(
        [
            output_weight.reshape(pointwise_in.shape[0], -1),
            pointwise_in,
            pointwise_out,
        ],
        axis=1,
    )
    late_weight = lax.all_gather(late_local, "dp", axis=0, tiled=True)
    out_cols = late_local.shape[1] - in_width - pointwise_out.shape[1]
    output_full = late_weight[:, :out_cols].reshape(-1, width)
    in_full = late_weight[:, out_cols : out_cols + in_width]
    out_full = late_weight[:, out_cols + in_width :]
    del out_rows
    half = KERNEL // 2
    middle = block_rows - 2 * EDGE

    def blocks_of(rows):
        return rows.reshape(blocks_here, block_rows, *rows.shape[1:])

    def edge_rows(rows):
        shaped = blocks_of(rows)
        return jnp.concatenate([shaped[:, :EDGE], shaped[:, block_rows - EDGE :]], axis=1)

    def middle_rows(rows):
        return blocks_of(rows)[:, EDGE : block_rows - EDGE]

    def frame_path(attended_rows, ordered_rows, valid_rows):
        count = attended_rows.shape[0] * attended_rows.shape[1]
        projected = add_rows(attended_rows.reshape(count, -1), output_full)
        after = (ordered_rows.reshape(count, width).astype(jnp.float32) + projected).astype(
            jnp.bfloat16
        )
        conv_normed = layer_norm(after, convolution_gain).astype(jnp.bfloat16)
        expanded = add_rows(conv_normed, in_full)
        gated = expanded[:, :width] * jax.nn.sigmoid(expanded[:, width:])
        gated = jnp.where(valid_rows.reshape(count)[:, None], gated, 0.0).astype(jnp.bfloat16)
        shape = attended_rows.shape[:2] + (width,)
        return after.reshape(shape), gated.reshape(shape)

    after_edge, edges = frame_path(edge_rows(attended), edge_rows(ordered), edge_rows(is_valid))
    all_edges = lax.all_gather(edges, "seq", axis=0, tiled=True)
    after_middle, gated_middle = frame_path(
        middle_rows(attended), middle_rows(ordered), middle_rows(is_valid)
    )
    gated_blocks = jnp.concatenate([edges[:, :EDGE], gated_middle, edges[:, EDGE:]], axis=1)
    after_blocks = jnp.concatenate(
        [after_edge[:, :EDGE], after_middle, after_edge[:, EDGE:]], axis=1
    )

    def convolve(padded, count):
        wide = lax.optimization_barrier(padded.astype(jnp.float32))
        total = jnp.zeros((blocks_here, count, width), jnp.float32)
        for tap in range(KERNEL):
            total = total + depthwise_taps[tap].astype(jnp.float32)[None, None, :] * wide[
                :, tap : tap + count
            ]
        return total

    def finish(depthwise, after):
        count = depthwise.shape[0] * depthwise.shape[1]
        shaped = layer_norm(depthwise.reshape(count, width), depthwise_gain)
        activated = (shaped * jax.nn.sigmoid(shaped)).astype(jnp.bfloat16)
        contracted = add_rows(activated, out_full)
        result = (after.reshape(count, width).astype(jnp.float32) + contracted).astype(
            jnp.bfloat16
        )
        return result.reshape(depthwise.shape)

    inner = finish(
        convolve(gated_blocks[:, EDGE - half :], middle), after_blocks[:, EDGE : block_rows - EDGE]
    )
    before = route_row[None, :] == (own_places[:, None] - 1)
    after = route_row[None, :] == (own_places[:, None] + 1)
    low = select_blocks(before, all_edges[:, EDGE:])[:, EDGE - half :]
    high = select_blocks(after, all_edges[:, :EDGE])[:, :half]
    low_conv = convolve(jnp.concatenate([low, gated_blocks[:, : EDGE + half]], axis=1), EDGE)
    high_conv = convolve(
        jnp.concatenate([gated_blocks[:, block_rows - EDGE - half :], high], axis=1), EDGE
    )
    outer = finish(
        jnp.concatenate([low_conv, high_conv], axis=1),
        jnp.concatenate([after_blocks[:, :EDGE], after_blocks[:, block_rows - EDGE :]], axis=1),
    )
    result = jnp.concatenate([outer[:, :EDGE], inner, outer[:, EDGE:]], axis=1)
    del middle
    return result[None]


def solution(mesh):
    placed = (
        P("dp", "seq", None, None),
        P("dp", None),
        P("dp"),
        P(),
        P("dp", None),
        P("dp", None),
        P("dp", None),
        P("dp", None),
        P(),
        P("dp", None),
        P(),
        P(),
        P("dp", None),
    )
    return jax.shard_map(
        body, mesh=mesh, in_specs=placed, out_specs=P("dp", "seq", None, None), check_vma=False
    )
```
